32 devices in a mesh: seq: 8 (over z, x), ep: 4 (over y, core).
Axes of the slice: x: 2, y: 2, z: 4, core: 2. Of those that a mesh axis runs over, the one named last changes fastest.
Arguments:
- queries: bfloat16 [4, 1024, 2048], P('ep', 'seq'), may hold values from -6 to 6
- key_rows: bfloat16 [4, 1024, 2048], P('ep', 'seq'), may hold values from -6 to 6
- value_rows: bfloat16 [4, 1024, 2048], P('ep', 'seq'), may hold values from -6 to 6
- residual: bfloat16 [4, 1024, 2048], P('ep', 'seq'), may hold values from -6 to 6
- state_start: float32 [4, 16, 128, 128], P('ep'), may hold values from -96 to 96
- head_gain: float32 [2048], replicated, may hold values from 0.25 to 1.75
- ffn_gain: float32 [2048], replicated, may hold values from 0.25 to 1.75
- routes: int32 [4, 1024, 6], P('ep', 'seq'), may hold values from 0 to 15, all different within a row; in each aligned block of 128 rows (0 to 127, 128 to 255, ..., all dimensions but the last counted through in order) at most 50 rows name the same one
- route_gates: float32 [4, 1024, 6], P('ep', 'seq'), may hold values from 0.1 to 1
- gate_weight: bfloat16 [16, 2048, 704], P('ep', 'seq'), may hold values from -0.125 to 0.125
- up_weight: bfloat16 [16, 2048, 704], P('ep', 'seq'), may hold values from -0.125 to 0.125
- down_weight: bfloat16 [16, 704, 2048], P('ep', None, 'seq'), may hold values from -0.21875 to 0.21875
Outputs:
- layer_out: bfloat16 [4, 1024, 2048], P('ep', 'seq')
The draws below stay inside these ranges and needn't reach their ends.
Inputs may be any that keep to these rules, and one draw needn't show every extreme that they name: `routes`: each position names 6 different experts. Among the positions of one device (aligned blocks of 128 positions) no expert is named more than 50 times, a bound that some block reaches.
All inputs are finite; a program needn't handle non-finite values.
Results may differ from the reference program's by a relative error of at most 0.015.
Values may be sent and summed in bfloat16 or wider, within the bound.
No kernel may reach another device: no remote copies, remote signals or barrier semaphores. Data moves between devices by JAX's collectives and lax.ppermute only.
A program may use at most 128 MiB of HBM per device.

```python
import math
import jax
import jax.numpy as jnp
import numpy as np
from jax import lax

D = 2048
HEADS = 16
HEAD_DIM = 128
HID = 704
EXPERTS = 16
TOP = 6
TOK_DEV = 128
CAP = 50
SEQS = 4
LENGTH = 1024
N_SEQ = 8


def block_scale(key, shape, cuts, smallest, largest):
    loudness, own = 1.0, jax.random.fold_in(key, 6)
    for axis_at, shards_of in cuts:
        draws = jnp.exp(jax.random.uniform(jax.random.fold_in(own, axis_at), (shards_of,), jnp.float32, smallest / len(cuts), largest / len(cuts)))
        loudness = loudness * jnp.repeat(draws, shape[axis_at] // shards_of).reshape([-1 if axis == axis_at else 1 for axis in range(len(shape))])
    return loudness


def shared_out(own_key, own, number, rows, number_of, top, bound, slope):
    order = jax.random.permutation(own_key, number_of)
    heavy_load, common = load_shares(number_of, rows * top, bound, slope, True), load_shares(number_of, rows * top, bound, slope, False)
    places = jnp.arange(number_of)

    def named(sizes, turn):
        used = int((sizes > 0).sum())
        fixed = max(1, used // 4)
        passed = fixed + (places - fixed + turn * (used - fixed)) % max(1, number_of - fixed)
        return jnp.zeros((number_of,), jnp.int32).at[order[jnp.where(places < fixed, places, passed)]].set(jnp.asarray(sizes, jnp.int32))

    sizes = jnp.where(number % 4 == 0, named(heavy_load, number // 4), named(common, number - number // 4 - 1))
    mixed = jax.random.permutation(jax.random.fold_in(own, 3), number_of)
    source_of, taker = mixed[0:number_of // 2 * 2:2], mixed[1:number_of // 2 * 2:2]
    margin = jnp.minimum(sizes[source_of] - 1, bound - sizes[taker]) // 2
    margin = jnp.where((source_of == order[0]) | (taker == order[0]) | (sizes[taker] == 0), 0, jnp.maximum(margin, 0))
    passed = jax.random.randint(jax.random.fold_in(own, 4), (number_of // 2,), 0, 1 << 20) % (margin + 1)
    sizes = sizes.at[source_of].add(-passed).at[taker].add(passed)
    members = jnp.searchsorted(jnp.cumsum(sizes), jnp.arange(rows * top), side="right").astype(jnp.int32)
    table = members.reshape(top, rows).T
    table = table[jax.random.permutation(jax.random.fold_in(own, 1), rows)]
    turn = jax.random.randint(jax.random.fold_in(own, 2), (rows, 1), 0, top)
    return jnp.take_along_axis(table, (jnp.arange(top)[None, :] + turn) % top, axis=1)


def load_shares(number_of, total, reach, slope, full):
    portions = [(1 << 20) // math.isqrt(rank ** slope) + 1 for rank in range(1, number_of + 1)]
    largest = reach if full else min(reach, max(-(-total // number_of), total * portions[0] // sum(portions)))
    least = 1 if total - largest >= number_of - 1 else 0
    holding, rest = [largest] + [least] * (number_of - 1), total - largest - least * (number_of - 1)
    while rest > 0:
        movable = [i for i in range(1, number_of) if holding[i] < largest] or [i for i in range(1, number_of) if holding[i] < reach]
        mass, remaining = sum([portions[i] for i in movable]), rest
        for i in movable:
            more = min(reach - holding[i], max(1, remaining * portions[i] // mass), rest)
            holding[i] = holding[i] + more
            rest = rest - more
    return np.array(holding)


def centred(rng, shape, spread, limit, shards=(), held_as=jnp.bfloat16):
    loudness = block_scale(rng, shape, shards, -0.22, 0.18) if shards else 1.0
    entries = jax.random.normal(rng, shape, jnp.float32) * spread * loudness
    return jnp.minimum(jnp.maximum(entries, -limit), limit).astype(held_as)


def setup_inputs(seed: int = 0) -> dict:
    streams_of = jax.random.split(jax.random.key(seed), 13)
    queries = centred(streams_of[0], (SEQS, LENGTH, D), 1.0, 6.0, ((0, 4), (1, 8)))
    key_rows = centred(streams_of[1], (SEQS, LENGTH, D), 1.0, 6.0, ((0, 4), (1, 8)))
    value_rows = centred(streams_of[2], (SEQS, LENGTH, D), 1.0, 6.0, ((0, 4), (1, 8)))
    residual = centred(streams_of[3], (SEQS, LENGTH, D), 1.0, 6.0, ((0, 4), (1, 8)))
    state_start = centred(streams_of[4], (SEQS, HEADS, HEAD_DIM, HEAD_DIM), (0.5 * LENGTH ** 0.5), 96.0, ((0, 4),), jnp.float32)
    head_gain = jnp.clip(1.0 + 0.15 * jax.random.normal(streams_of[5], (D,), jnp.float32), 0.25, 1.75)
    ffn_gain = jnp.clip(1.0 + 0.15 * jax.random.normal(streams_of[6], (D,), jnp.float32), 0.25, 1.75)
    routes_keys = jax.random.split(jax.random.fold_in(streams_of[7], 1), SEQS * LENGTH // TOK_DEV)
    routes_turns = jax.random.permutation(jax.random.fold_in(streams_of[7], 3), SEQS * LENGTH // TOK_DEV)
    routes = jax.vmap(lambda own, number: shared_out(jax.random.fold_in(streams_of[7], 2), own, number, TOK_DEV, EXPERTS, TOP, CAP, 2))(routes_keys, routes_turns).reshape((SEQS, LENGTH, TOP))
    route_gates = jnp.clip(0.1 + 0.9 * jax.random.uniform(streams_of[8], (SEQS, LENGTH, TOP), jnp.float32) ** block_scale(streams_of[8], (SEQS, LENGTH, TOP), ((0, 4), (1, 8)), -0.2, 0.2), 0.1, 1.0)
    gate_weight = centred(streams_of[9], (EXPERTS, D, HID), D ** -0.5, 0.125, ((0, 4), (1, 8)))
    up_weight = centred(streams_of[10], (EXPERTS, D, HID), D ** -0.5, 0.125, ((0, 4), (1, 8)))
    down_weight = centred(streams_of[11], (EXPERTS, HID, D), HID ** -0.5, 0.21875, ((0, 4), (2, 8)))
    return {"queries": queries, "key_rows": key_rows, "value_rows": value_rows, "residual": residual, "state_start": state_start, "head_gain": head_gain, "ffn_gain": ffn_gain, "routes": routes, "route_gates": route_gates, "gate_weight": gate_weight, "up_weight": up_weight, "down_weight": down_weight}


def route_slots(block_routes):
    chosen = (block_routes[:, None] == jnp.arange(EXPERTS, dtype=jnp.int32)[None, :]).astype(jnp.int32)
    counts = jnp.cumsum(chosen, axis=0) - 1
    return lax.optimization_barrier(jnp.sum(chosen * counts, axis=1)).astype(jnp.int32)

def silu_gate(gate_sum, up_sum):
    return gate_sum / (1.0 + jnp.exp(-gate_sum)) * up_sum

def reference(queries, key_rows, value_rows, residual, state_start, head_gain, ffn_gain, routes, route_gates, gate_weight, up_weight, down_weight):
    highest = lax.Precision.HIGHEST
    causal = jnp.arange(TOK_DEV, dtype=jnp.int32)[:, None] >= jnp.arange(TOK_DEV, dtype=jnp.int32)[None, :]

    def attend_block(state_before, block):
        query_heads, key_heads, value_heads = block
        query_wide = query_heads.astype(jnp.float32)
        key_wide = key_heads.astype(jnp.float32)
        value_wide = value_heads.astype(jnp.float32)
        from_state = jnp.einsum('thd,hde->the', query_wide, state_before, precision=highest)
        scores = jnp.einsum('thd,shd->hts', query_wide, key_wide, precision=highest)
        scores = jnp.where(causal[None], scores, 0.0).astype(jnp.bfloat16)
        in_block = jnp.einsum('hts,she->the', scores.astype(jnp.float32), value_wide, precision=highest)
        state_after = state_before + jnp.einsum('thd,the->hde', key_wide, value_wide, precision=highest)
        return (state_after, from_state + in_block)

    def run_expert(packed_expert):
        rows, gate_part, up_part, down_part = packed_expert
        gate_sum = jnp.dot(rows, gate_part, preferred_element_type=jnp.float32)
        up_sum = jnp.dot(rows, up_part, preferred_element_type=jnp.float32)
        hidden = silu_gate(gate_sum, up_sum).astype(jnp.bfloat16)
        return jnp.dot(hidden, down_part, preferred_element_type=jnp.float32).astype(jnp.bfloat16)

    def one_sequence(packed):
        query_seq, key_seq, value_seq, resid_seq, state_seq, route_seq, weight_seq = packed
        blocked = (query_seq.reshape(N_SEQ, TOK_DEV, HEADS, HEAD_DIM), key_seq.reshape(N_SEQ, TOK_DEV, HEADS, HEAD_DIM), value_seq.reshape(N_SEQ, TOK_DEV, HEADS, HEAD_DIM))
        final_state, attended = lax.scan(attend_block, state_seq, blocked)
        attended = attended.reshape(LENGTH, HEADS, HEAD_DIM)
        head_scale = lax.rsqrt(lax.optimization_barrier(jnp.mean(attended * attended, axis=-1, keepdims=True)) + 1e-05)
        head_normed = (attended * head_scale).reshape(LENGTH, D) * head_gain
        mixed_rows = (resid_seq.astype(jnp.float32) + head_normed).astype(jnp.bfloat16)
        mixed_rows = lax.optimization_barrier(mixed_rows)
        mixed_wide = mixed_rows.astype(jnp.float32)
        row_scale = lax.rsqrt(lax.optimization_barrier(jnp.mean(mixed_wide * mixed_wide, axis=-1, keepdims=True)) + 1e-05)
        ffn_in = (mixed_wide * row_scale * ffn_gain).astype(jnp.bfloat16)
        flat_routes = route_seq.reshape(N_SEQ, TOK_DEV * TOP)
        slot_rank = jax.vmap(route_slots)(flat_routes)
        block_index = jnp.arange(N_SEQ, dtype=jnp.int32)[:, None]
        position = (flat_routes * (N_SEQ * CAP) + block_index * CAP + slot_rank).reshape(-1)
        token_index = (block_index * TOK_DEV + jnp.arange(TOK_DEV * TOP, dtype=jnp.int32)[None, :] // TOP).reshape(-1)
        source = jnp.zeros((EXPERTS * N_SEQ * CAP,), jnp.int32).at[position].set(token_index)
        filled = jnp.zeros((EXPERTS * N_SEQ * CAP,), jnp.bool_).at[position].set(True)
        buffers = jnp.where(filled[:, None], ffn_in[source], jnp.zeros((), jnp.bfloat16)).reshape(EXPERTS, N_SEQ * CAP, D)
        outputs = lax.map(run_expert, (buffers, gate_weight, up_weight, down_weight))
        picked = outputs.reshape(EXPERTS * N_SEQ * CAP, D)[position].reshape(LENGTH, TOP, D)
        expert_mix = lax.optimization_barrier(jnp.sum(weight_seq[:, :, None] * picked.astype(jnp.float32), axis=1))
        return (mixed_wide + expert_mix).astype(jnp.bfloat16)
    return lax.map(one_sequence, (queries, key_rows, value_rows, residual, state_start, routes, route_gates))
```

```python
import jax
import jax.numpy as jnp
from jax import lax
from jax.sharding import PartitionSpec as P

D = 2048
HEADS = 16
HEAD_DIM = 128
EXPERTS = 16
TOP = 6
CAP = 50


def carried_in(array, axis, join, neutral):
    place = lax.axis_index(axis)
    gathered = lax.all_gather(array.astype(jnp.bfloat16), axis)
    state = jnp.zeros_like(array) + jnp.asarray(neutral, array.dtype)

    def one(turn, state):
        return join(state, lax.dynamic_index_in_dim(gathered, turn, 0, False).astype(array.dtype))

    return lax.fori_loop(0, place, one, state)


def route_slots(block_routes):
    chosen = (block_routes[:, None] == jnp.arange(EXPERTS, dtype=jnp.int32)[None, :]).astype(
        jnp.int32
    )
    counts = jnp.cumsum(chosen, axis=0) - 1
    return jnp.sum(chosen * counts, axis=1)


def silu_gate(gate_sum, up_sum):
    return gate_sum / (1.0 + jnp.exp(-gate_sum)) * up_sum


def add_states(earlier, later):
    return earlier + later


def make_shards(n_ep, n_seq):
    n_dev = n_ep * n_seq

    def shards(
        queries,
        key_rows,
        value_rows,
        residual,
        state_start,
        head_gain,
        ffn_gain,
        routes,
        route_gates,
        gate_weight,
        up_weight,
        down_weight,
    ):
        local_experts = gate_weight.shape[0]
        per = n_seq // local_experts
        chunk = -(-CAP // per)
        capp = chunk * per

        seq_place = lax.axis_index("seq")
        wanted = jnp.arange(n_seq, dtype=jnp.int32) // per
        whole_gate = lax.all_to_all(gate_weight[wanted], "seq", 0, 0, tiled=True)
        whole_up = lax.all_to_all(up_weight[wanted], "seq", 0, 0, tiled=True)
        whole_down = lax.all_to_all(down_weight[wanted], "seq", 0, 0, tiled=True)
        whole_gate = whole_gate.reshape(-1, whole_gate.shape[-1])
        whole_up = whole_up.reshape(-1, whole_up.shape[-1])

        tokens = queries.shape[1]
        query_heads = queries[0].reshape(tokens, HEADS, HEAD_DIM)
        key_heads = key_rows[0].reshape(tokens, HEADS, HEAD_DIM)
        value_heads = value_rows[0].reshape(tokens, HEADS, HEAD_DIM)
        local_state = jnp.einsum(
            "thd,the->hde", key_heads, value_heads, preferred_element_type=jnp.float32
        )
        earlier = carried_in(local_state, "seq", add_states, jnp.zeros_like(local_state))
        state_before = state_start[0] + earlier
        causal = (
            jnp.arange(tokens, dtype=jnp.int32)[:, None]
            >= jnp.arange(tokens, dtype=jnp.int32)[None, :]
        )
        scores = jnp.einsum(
            "thd,shd->hts", query_heads, key_heads, preferred_element_type=jnp.float32
        )
        scores = jnp.where(causal[None], scores, 0.0).astype(jnp.bfloat16)
        in_block = jnp.einsum(
            "hts,she->the", scores, value_heads, preferred_element_type=jnp.float32
        )
        from_state = jnp.einsum(
            "thd,hde->the",
            query_heads.astype(jnp.float32),
            state_before,
            precision=lax.Precision.HIGHEST,
        )
        attended = from_state + in_block
        head_scale = lax.rsqrt(jnp.mean(attended * attended, axis=-1, keepdims=True) + 1e-05)
        head_normed = (attended * head_scale).reshape(tokens, D) * head_gain
        mixed_rows = (residual[0].astype(jnp.float32) + head_normed).astype(jnp.bfloat16)
        mixed_rows = lax.optimization_barrier(mixed_rows)
        mixed_wide = mixed_rows.astype(jnp.float32)
        row_scale = lax.rsqrt(jnp.mean(mixed_wide * mixed_wide, axis=-1, keepdims=True) + 1e-05)
        ffn_in = (mixed_wide * row_scale * ffn_gain).astype(jnp.bfloat16)
        flat_routes = routes[0].reshape(-1)
        slot_rank = route_slots(flat_routes)
        position = flat_routes * capp + slot_rank
        token_index = jnp.arange(tokens * TOP, dtype=jnp.int32) // TOP
        source = jnp.zeros((EXPERTS * capp,), jnp.int32).at[position].set(token_index)
        filled = jnp.zeros((EXPERTS * capp,), jnp.bool_).at[position].set(True)
        outgoing = jnp.where(filled[:, None], ffn_in[source], jnp.zeros((), jnp.bfloat16))
        outgoing = outgoing.reshape(EXPERTS * per, chunk, D)
        arrived = lax.all_to_all(outgoing, ("ep", "seq"), 0, 0, tiled=True)
        arrived = arrived.reshape(n_dev * chunk, D)
        gate_sum = jnp.dot(arrived, whole_gate, preferred_element_type=jnp.float32)
        up_sum = jnp.dot(arrived, whole_up, preferred_element_type=jnp.float32)
        hidden = silu_gate(gate_sum, up_sum).astype(jnp.bfloat16)
        expert_rows = jnp.einsum(
            "rh,shd->rsd", hidden, whole_down, preferred_element_type=jnp.float32
        ).astype(jnp.bfloat16)
        expert_rows = expert_rows.reshape(n_dev, chunk, D)
        returned = lax.all_to_all(expert_rows, ("ep", "seq"), 0, 0, tiled=True)
        picked = returned.reshape(EXPERTS * capp, D)[position].reshape(tokens, TOP, D)
        expert_mix = jnp.sum(route_gates[0][:, :, None] * picked.astype(jnp.float32), axis=1)
        del seq_place
        return (mixed_wide + expert_mix).astype(jnp.bfloat16)[None]

    return shards


def solution(mesh):
    placed = (
        P("ep", "seq", None),
        P("ep", "seq", None),
        P("ep", "seq", None),
        P("ep", "seq", None),
        P("ep", None, None, None),
        P(),
        P(),
        P("ep", "seq", None),
        P("ep", "seq", None),
        P("ep", "seq", None),
        P("ep", "seq", None),
        P("ep", None, "seq"),
    )
    shards = make_shards(mesh.shape["ep"], mesh.shape["seq"])
    return jax.shard_map(
        shards, mesh=mesh, in_specs=placed, out_specs=P("ep", "seq", None), check_vma=False
    )
```

```python
import jax
import jax.numpy as jnp
from jax import lax
from jax.sharding import PartitionSpec as P

D = 2048
HEADS = 16
HEAD_DIM = 128
EXPERTS = 16
TOP = 6
CAP = 50


def carried_in(array, axis, join, neutral):
    place = lax.axis_index(axis)
    gathered = lax.all_gather(array.astype(jnp.bfloat16), axis)
    state = jnp.zeros_like(array) + jnp.asarray(neutral, array.dtype)

    def one(turn, state):
        return join(state, lax.dynamic_index_in_dim(gathered, turn, 0, False).astype(array.dtype))

    return lax.fori_loop(0, place, one, state)


def route_slots(block_routes):
    chosen = (block_routes[:, None] == jnp.arange(EXPERTS, dtype=jnp.int32)[None, :]).astype(
        jnp.int32
    )
    counts = jnp.cumsum(chosen, axis=0) - 1
    return jnp.sum(chosen * counts, axis=1)


def silu_gate(gate_sum, up_sum):
    return gate_sum / (1.0 + jnp.exp(-gate_sum)) * up_sum


def add_states(earlier, later):
    return earlier + later


def make_shards(n_ep, n_seq):
    n_dev = n_ep * n_seq

    def shards(
        queries,
        key_rows,
        value_rows,
        residual,
        state_start,
        head_gain,
        ffn_gain,
        routes,
        route_gates,
        gate_weight,
        up_weight,
        down_weight,
    ):
        local_experts = gate_weight.shape[0]
        per = n_seq // local_experts
        chunk = -(-CAP // per)
        capp = chunk * per

        seq_place = lax.axis_index("seq")
        slice_rows, hid = gate_weight.shape[1], gate_weight.shape[2]
        part = slice_rows * hid
        packed = jnp.concatenate(
            [
                gate_weight.reshape(local_experts, part),
                up_weight.reshape(local_experts, part),
                down_weight.reshape(local_experts, part),
            ],
            axis=1,
        )
        pieces = [lax.dynamic_index_in_dim(packed, seq_place // per, 0, False)]
        for turn in range(1, n_seq):
            target = (seq_place - turn) % n_seq
            pieces.append(
                lax.ppermute(
                    lax.dynamic_index_in_dim(packed, target // per, 0, False),
                    "seq",
                    [(i, (i - turn) % n_seq) for i in range(n_seq)],
                )
            )
        whole = jnp.roll(jnp.stack(pieces), seq_place, axis=0)
        whole_gate = whole[:, :part].reshape(n_seq * slice_rows, hid)
        whole_up = whole[:, part : 2 * part].reshape(n_seq * slice_rows, hid)
        whole_down = whole[:, 2 * part :].reshape(n_seq, hid, slice_rows)

        tokens = queries.shape[1]
        query_heads = queries[0].reshape(tokens, HEADS, HEAD_DIM)
        key_heads = key_rows[0].reshape(tokens, HEADS, HEAD_DIM)
        value_heads = value_rows[0].reshape(tokens, HEADS, HEAD_DIM)
        local_state = jnp.einsum(
            "thd,the->hde", key_heads, value_heads, preferred_element_type=jnp.float32
        )
        earlier = carried_in(local_state, "seq", add_states, jnp.zeros_like(local_state))
        state_before = state_start[0] + earlier
        causal = (
            jnp.arange(tokens, dtype=jnp.int32)[:, None]
            >= jnp.arange(tokens, dtype=jnp.int32)[None, :]
        )
        scores = jnp.einsum(
            "thd,shd->hts", query_heads, key_heads, preferred_element_type=jnp.float32
        )
        scores = jnp.where(causal[None], scores, 0.0).astype(jnp.bfloat16)
        in_block = jnp.einsum(
            "hts,she->the", scores, value_heads, preferred_element_type=jnp.float32
        )
        from_state = jnp.einsum(
            "thd,hde->the",
            query_heads.astype(jnp.float32),
            state_before,
            precision=lax.Precision.HIGHEST,
        )
        attended = from_state + in_block
        head_scale = lax.rsqrt(jnp.mean(attended * attended, axis=-1, keepdims=True) + 1e-05)
        head_normed = (attended * head_scale).reshape(tokens, D) * head_gain
        mixed_rows = (residual[0].astype(jnp.float32) + head_normed).astype(jnp.bfloat16)
        mixed_rows = lax.optimization_barrier(mixed_rows)
        mixed_wide = mixed_rows.astype(jnp.float32)
        row_scale = lax.rsqrt(jnp.mean(mixed_wide * mixed_wide, axis=-1, keepdims=True) + 1e-05)
        ffn_in = (mixed_wide * row_scale * ffn_gain).astype(jnp.bfloat16)
        flat_routes = routes[0].reshape(-1)
        slot_rank = route_slots(flat_routes)
        position = flat_routes * capp + slot_rank
        token_index = jnp.arange(tokens * TOP, dtype=jnp.int32) // TOP
        source = jnp.zeros((EXPERTS * capp,), jnp.int32).at[position].set(token_index)
        filled = jnp.zeros((EXPERTS * capp,), jnp.bool_).at[position].set(True)
        outgoing = jnp.where(filled[:, None], ffn_in[source], jnp.zeros((), jnp.bfloat16))
        outgoing = outgoing.reshape(EXPERTS * per, chunk, D)
        arrived = lax.all_to_all(outgoing, ("ep", "seq"), 0, 0, tiled=True)
        arrived = arrived.reshape(n_dev * chunk, D)
        gate_sum = jnp.dot(arrived, whole_gate, preferred_element_type=jnp.float32)
        up_sum = jnp.dot(arrived, whole_up, preferred_element_type=jnp.float32)
        hidden = silu_gate(gate_sum, up_sum).astype(jnp.bfloat16)
        expert_rows = jnp.einsum(
            "rh,shd->rsd", hidden, whole_down, preferred_element_type=jnp.float32
        ).astype(jnp.bfloat16)
        expert_rows = expert_rows.reshape(n_dev, chunk, D)
        returned = lax.all_to_all(expert_rows, ("ep", "seq"), 0, 0, tiled=True)
        picked = returned.reshape(EXPERTS * capp, D)[position].reshape(tokens, TOP, D)
        expert_mix = jnp.sum(route_gates[0][:, :, None] * picked.astype(jnp.float32), axis=1)
        del seq_place
        return (mixed_wide + expert_mix).astype(jnp.bfloat16)[None]

    return shards


def solution(mesh):
    placed = (
        P("ep", "seq", None),
        P("ep", "seq", None),
        P("ep", "seq", None),
        P("ep", "seq", None),
        P("ep", None, None, None),
        P(),
        P(),
        P("ep", "seq", None),
        P("ep", "seq", None),
        P("ep", "seq", None),
        P("ep", "seq", None),
        P("ep", None, "seq"),
    )
    shards = make_shards(mesh.shape["ep"], mesh.shape["seq"])
    return jax.shard_map(
        shards, mesh=mesh, in_specs=placed, out_specs=P("ep", "seq", None), check_vma=False
    )
```

```python
import jax
import jax.numpy as jnp
from jax import lax
from jax.sharding import Mesh, PartitionSpec as P

D = 2048
HEADS = 16
HEAD_DIM = 128
EXPERTS = 16
TOP = 6
CAP = 50


def carried_in(array, axis, join, neutral):
    place = lax.axis_index(axis)
    gathered = lax.all_gather(array.astype(jnp.bfloat16), axis)
    state = jnp.zeros_like(array) + jnp.asarray(neutral, array.dtype)

    def one(turn, state):
        return join(state, lax.dynamic_index_in_dim(gathered, turn, 0, False).astype(array.dtype))

    return lax.fori_loop(0, place, one, state)


def route_slots(block_routes):
    chosen = (block_routes[:, None] == jnp.arange(EXPERTS, dtype=jnp.int32)[None, :]).astype(
        jnp.int32
    )
    counts = jnp.cumsum(chosen, axis=0) - 1
    return jnp.sum(chosen * counts, axis=1)


def silu_gate(gate_sum, up_sum):
    return gate_sum / (1.0 + jnp.exp(-gate_sum)) * up_sum


def add_states(earlier, later):
    return earlier + later


def make_shards(n_ep, n_outer, n_inner):
    n_seq = n_outer * n_inner
    n_dev = n_ep * n_seq

    def shards(
        queries,
        key_rows,
        value_rows,
        residual,
        state_start,
        head_gain,
        ffn_gain,
        routes,
        route_gates,
        gate_weight,
        up_weight,
        down_weight,
    ):
        local_experts = gate_weight.shape[0]
        per = n_seq // local_experts
        chunk = -(-CAP // per)
        capp = chunk * per

        per_outer = n_outer // local_experts
        wanted = jnp.arange(n_outer, dtype=jnp.int32) // per_outer

        def collect(weight):
            mine = lax.all_to_all(weight[wanted], "seq_outer", 0, 0, tiled=True)
            return lax.all_gather(mine, "seq_inner", axis=0, tiled=False)

        whole_gate = collect(gate_weight)
        whole_up = collect(up_weight)
        whole_down = collect(down_weight)
        whole_gate = whole_gate.reshape(-1, whole_gate.shape[-1])
        whole_up = whole_up.reshape(-1, whole_up.shape[-1])

        tokens = queries.shape[1]
        query_heads = queries[0].reshape(tokens, HEADS, HEAD_DIM)
        key_heads = key_rows[0].reshape(tokens, HEADS, HEAD_DIM)
        value_heads = value_rows[0].reshape(tokens, HEADS, HEAD_DIM)
        local_state = jnp.einsum(
            "thd,the->hde", key_heads, value_heads, preferred_element_type=jnp.float32
        )
        earlier = carried_in(local_state, ("seq_outer", "seq_inner"), add_states, jnp.zeros_like(local_state))
        state_before = state_start[0] + earlier
        causal = (
            jnp.arange(tokens, dtype=jnp.int32)[:, None]
            >= jnp.arange(tokens, dtype=jnp.int32)[None, :]
        )
        scores = jnp.einsum(
            "thd,shd->hts", query_heads, key_heads, preferred_element_type=jnp.float32
        )
        scores = jnp.where(causal[None], scores, 0.0).astype(jnp.bfloat16)
        in_block = jnp.einsum(
            "hts,she->the", scores, value_heads, preferred_element_type=jnp.float32
        )
        from_state = jnp.einsum(
            "thd,hde->the",
            query_heads.astype(jnp.float32),
            state_before,
            precision=lax.Precision.HIGHEST,
        )
        attended = from_state + in_block
        head_scale = lax.rsqrt(jnp.mean(attended * attended, axis=-1, keepdims=True) + 1e-05)
        head_normed = (attended * head_scale).reshape(tokens, D) * head_gain
        mixed_rows = (residual[0].astype(jnp.float32) + head_normed).astype(jnp.bfloat16)
        mixed_rows = lax.optimization_barrier(mixed_rows)
        mixed_wide = mixed_rows.astype(jnp.float32)
        row_scale = lax.rsqrt(jnp.mean(mixed_wide * mixed_wide, axis=-1, keepdims=True) + 1e-05)
        ffn_in = (mixed_wide * row_scale * ffn_gain).astype(jnp.bfloat16)
        flat_routes = routes[0].reshape(-1)
        slot_rank = route_slots(flat_routes)
        position = flat_routes * capp + slot_rank
        token_index = jnp.arange(tokens * TOP, dtype=jnp.int32) // TOP
        source = jnp.zeros((EXPERTS * capp,), jnp.int32).at[position].set(token_index)
        filled = jnp.zeros((EXPERTS * capp,), jnp.bool_).at[position].set(True)
        outgoing = jnp.where(filled[:, None], ffn_in[source], jnp.zeros((), jnp.bfloat16))
        outgoing = outgoing.reshape(EXPERTS * per, chunk, D)
        arrived = lax.all_to_all(outgoing, ("ep", "seq_outer", "seq_inner"), 0, 0, tiled=True)
        arrived = arrived.reshape(n_dev * chunk, n_outer, n_inner, D // n_seq)
        arrived = arrived.transpose(0, 2, 1, 3).reshape(n_dev * chunk, D)
        gate_sum = jnp.dot(arrived, whole_gate, preferred_element_type=jnp.float32)
        up_sum = jnp.dot(arrived, whole_up, preferred_element_type=jnp.float32)
        hidden = silu_gate(gate_sum, up_sum).astype(jnp.bfloat16)
        expert_rows = jnp.einsum(
            "rh,xzhd->rzxd", hidden, whole_down, preferred_element_type=jnp.float32
        ).astype(jnp.bfloat16)
        expert_rows = expert_rows.reshape(n_dev, chunk, D)
        returned = lax.all_to_all(expert_rows, ("ep", "seq_outer", "seq_inner"), 0, 0, tiled=True)
        picked = returned.reshape(EXPERTS * capp, D)[position].reshape(tokens, TOP, D)
        expert_mix = jnp.sum(route_gates[0][:, :, None] * picked.astype(jnp.float32), axis=1)
        return (mixed_wide + expert_mix).astype(jnp.bfloat16)[None]

    return shards


def solution(mesh):
    seq = ("seq_outer", "seq_inner")
    placed = (
        P("ep", seq, None),
        P("ep", seq, None),
        P("ep", seq, None),
        P("ep", seq, None),
        P("ep", None, None, None),
        P(),
        P(),
        P("ep", seq, None),
        P("ep", seq, None),
        P("ep", seq, None),
        P("ep", seq, None),
        P("ep", None, seq),
    )
    n_seq, n_ep = mesh.shape["seq"], mesh.shape["ep"]
    n_inner = 2 if n_seq % 2 == 0 else 1
    names = list(mesh.axis_names)
    shape = []
    for name in names:
        shape += [n_seq // n_inner, n_inner] if name == "seq" else [mesh.shape[name]]
    split_names = []
    for name in names:
        split_names += list(seq) if name == "seq" else [name]
    split = Mesh(mesh.devices.reshape(shape), tuple(split_names))
    shards = make_shards(n_ep, n_seq // n_inner, n_inner)
    return jax.shard_map(
        shards, mesh=split, in_specs=placed, out_specs=P("ep", seq, None), check_vma=False
    )
```

```python
import jax
import jax.numpy as jnp
from jax import lax
from jax.sharding import Mesh, PartitionSpec as P

D = 2048
HEADS = 16
HEAD_DIM = 128
EXPERTS = 16
TOP = 6
CAP = 50


def carried_in(array, axis, count):
    total = array
    shift = 1
    while shift < count:
        moved = lax.ppermute(total, axis, [(i, i + shift) for i in range(count - shift)])
        total = total + moved
        shift *= 2
    return total - array


def route_slots(block_routes):
    chosen = (block_routes[:, None] == jnp.arange(EXPERTS, dtype=jnp.int32)[None, :]).astype(
        jnp.int32
    )
    counts = jnp.cumsum(chosen, axis=0) - 1
    return jnp.sum(chosen * counts, axis=1)


def silu_gate(gate_sum, up_sum):
    return gate_sum / (1.0 + jnp.exp(-gate_sum)) * up_sum


def make_shards(n_ep, n_outer, n_inner):
    n_seq = n_outer * n_inner
    n_dev = n_ep * n_seq

    def shards(
        queries,
        key_rows,
        value_rows,
        residual,
        state_start,
        head_gain,
        ffn_gain,
        routes,
        route_gates,
        gate_weight,
        up_weight,
        down_weight,
    ):
        local_experts = gate_weight.shape[0]
        per = n_seq // local_experts
        chunk = -(-CAP // per)
        capp = chunk * per

        per_outer = n_outer // local_experts
        wanted = jnp.arange(n_outer, dtype=jnp.int32) // per_outer

        def collect(weight):
            mine = lax.all_to_all(weight[wanted], "seq_outer", 0, 0, tiled=True)
            return lax.all_gather(mine, "seq_inner", axis=0, tiled=False)

        whole_gate = collect(gate_weight)
        whole_up = collect(up_weight)
        whole_down = collect(down_weight)
        whole_gate = whole_gate.reshape(-1, whole_gate.shape[-1])
        whole_up = whole_up.reshape(-1, whole_up.shape[-1])

        tokens = queries.shape[1]
        query_heads = queries[0].reshape(tokens, HEADS, HEAD_DIM)
        key_heads = key_rows[0].reshape(tokens, HEADS, HEAD_DIM)
        value_heads = value_rows[0].reshape(tokens, HEADS, HEAD_DIM)
        local_state = jnp.einsum(
            "thd,the->hde", key_heads, value_heads, preferred_element_type=jnp.float32
        )
        earlier = carried_in(local_state, ("seq_outer", "seq_inner"), n_seq)
        state_before = state_start[0] + earlier
        causal = (
            jnp.arange(tokens, dtype=jnp.int32)[:, None]
            >= jnp.arange(tokens, dtype=jnp.int32)[None, :]
        )
        scores = jnp.einsum(
            "thd,shd->hts", query_heads, key_heads, preferred_element_type=jnp.float32
        )
        scores = jnp.where(causal[None], scores, 0.0).astype(jnp.bfloat16)
        in_block = jnp.einsum(
            "hts,she->the", scores, value_heads, preferred_element_type=jnp.float32
        )
        from_state = jnp.einsum(
            "thd,hde->the",
            query_heads.astype(jnp.float32),
            state_before,
            precision=lax.Precision.HIGHEST,
        )
        attended = from_state + in_block
        head_scale = lax.rsqrt(jnp.mean(attended * attended, axis=-1, keepdims=True) + 1e-05)
        head_normed = (attended * head_scale).reshape(tokens, D) * head_gain
        mixed_rows = (residual[0].astype(jnp.float32) + head_normed).astype(jnp.bfloat16)
        mixed_rows = lax.optimization_barrier(mixed_rows)
        mixed_wide = mixed_rows.astype(jnp.float32)
        row_scale = lax.rsqrt(jnp.mean(mixed_wide * mixed_wide, axis=-1, keepdims=True) + 1e-05)
        ffn_in = (mixed_wide * row_scale * ffn_gain).astype(jnp.bfloat16)
        flat_routes = routes[0].reshape(-1)
        slot_rank = route_slots(flat_routes)
        position = flat_routes * capp + slot_rank
        token_index = jnp.arange(tokens * TOP, dtype=jnp.int32) // TOP
        source = jnp.zeros((EXPERTS * capp,), jnp.int32).at[position].set(token_index)
        filled = jnp.zeros((EXPERTS * capp,), jnp.bool_).at[position].set(True)
        outgoing = jnp.where(filled[:, None], ffn_in[source], jnp.zeros((), jnp.bfloat16))
        outgoing = outgoing.reshape(EXPERTS * per, chunk, D)
        arrived = lax.all_to_all(outgoing, ("ep", "seq_outer", "seq_inner"), 0, 0, tiled=True)
        arrived = arrived.reshape(n_dev * chunk, n_outer, n_inner, D // n_seq)
        arrived = arrived.transpose(0, 2, 1, 3).reshape(n_dev * chunk, D)
        gate_sum = jnp.dot(arrived, whole_gate, preferred_element_type=jnp.float32)
        up_sum = jnp.dot(arrived, whole_up, preferred_element_type=jnp.float32)
        hidden = silu_gate(gate_sum, up_sum).astype(jnp.bfloat16)
        expert_rows = jnp.einsum(
            "rh,xzhd->rzxd", hidden, whole_down, preferred_element_type=jnp.float32
        ).astype(jnp.bfloat16)
        expert_rows = expert_rows.reshape(n_dev, chunk, D)
        returned = lax.all_to_all(expert_rows, ("ep", "seq_outer", "seq_inner"), 0, 0, tiled=True)
        picked = returned.reshape(EXPERTS * capp, D)[position].reshape(tokens, TOP, D)
        expert_mix = jnp.sum(route_gates[0][:, :, None] * picked.astype(jnp.float32), axis=1)
        return (mixed_wide + expert_mix).astype(jnp.bfloat16)[None]

    return shards


def solution(mesh):
    seq = ("seq_outer", "seq_inner")
    placed = (
        P("ep", seq, None),
        P("ep", seq, None),
        P("ep", seq, None),
        P("ep", seq, None),
        P("ep", None, None, None),
        P(),
        P(),
        P("ep", seq, None),
        P("ep", seq, None),
        P("ep", seq, None),
        P("ep", seq, None),
        P("ep", None, seq),
    )
    n_seq, n_ep = mesh.shape["seq"], mesh.shape["ep"]
    n_inner = 2 if n_seq % 2 == 0 else 1
    names = list(mesh.axis_names)
    shape = []
    for name in names:
        shape += [n_seq // n_inner, n_inner] if name == "seq" else [mesh.shape[name]]
    split_names = []
    for name in names:
        split_names += list(seq) if name == "seq" else [name]
    split = Mesh(mesh.devices.reshape(shape), tuple(split_names))
    shards = make_shards(n_ep, n_seq // n_inner, n_inner)
    return jax.shard_map(
        shards, mesh=split, in_specs=placed, out_specs=P("ep", seq, None), check_vma=False
    )
```

```python
import jax
import jax.numpy as jnp
from jax import lax
from jax.sharding import Mesh, PartitionSpec as P

D = 2048
HEADS = 16
HEAD_DIM = 128
EXPERTS = 16
TOP = 6
CAP = 50


def carried_in(array, axis, count):
    total = array
    shift = 1
    while shift < count:
        moved = lax.ppermute(total, axis, [(i, i + shift) for i in range(count - shift)])
        total = total + moved
        shift *= 2
    return total - array


def route_slots(block_routes):
    chosen = (block_routes[:, None] == jnp.arange(EXPERTS, dtype=jnp.int32)[None, :]).astype(
        jnp.int32
    )
    counts = jnp.cumsum(chosen, axis=0) - 1
    return jnp.sum(chosen * counts, axis=1)


def silu_gate(gate_sum, up_sum):
    return gate_sum / (1.0 + jnp.exp(-gate_sum)) * up_sum


def make_shards(n_ep, n_outer, n_inner):
    n_seq = n_outer * n_inner
    n_dev = n_ep * n_seq

    def shards(
        queries,
        key_rows,
        value_rows,
        residual,
        state_start,
        head_gain,
        ffn_gain,
        routes,
        route_gates,
        gate_weight,
        up_weight,
        down_weight,
    ):
        local_experts = gate_weight.shape[0]
        per = n_seq // local_experts
        chunk = -(-CAP // per)
        capp = chunk * per

        tokens = queries.shape[1]
        query_heads = queries[0].reshape(tokens, HEADS, HEAD_DIM)
        key_heads = key_rows[0].reshape(tokens, HEADS, HEAD_DIM)
        value_heads = value_rows[0].reshape(tokens, HEADS, HEAD_DIM)
        local_state = jnp.einsum(
            "thd,the->hde", key_heads, value_heads, preferred_element_type=jnp.float32
        )
        earlier = carried_in(local_state, ("seq_outer", "seq_inner"), n_seq)
        state_before = state_start[0] + earlier
        causal = (
            jnp.arange(tokens, dtype=jnp.int32)[:, None]
            >= jnp.arange(tokens, dtype=jnp.int32)[None, :]
        )
        scores = jnp.einsum(
            "thd,shd->hts", query_heads, key_heads, preferred_element_type=jnp.float32
        )
        scores = jnp.where(causal[None], scores, 0.0).astype(jnp.bfloat16)
        in_block = jnp.einsum(
            "hts,she->the", scores, value_heads, preferred_element_type=jnp.float32
        )
        from_state = jnp.einsum(
            "thd,hde->the",
            query_heads.astype(jnp.float32),
            state_before,
            precision=lax.Precision.HIGHEST,
        )
        attended = from_state + in_block
        head_scale = lax.rsqrt(jnp.mean(attended * attended, axis=-1, keepdims=True) + 1e-05)
        head_normed = (attended * head_scale).reshape(tokens, D) * head_gain
        mixed_rows = (residual[0].astype(jnp.float32) + head_normed).astype(jnp.bfloat16)
        mixed_rows = lax.optimization_barrier(mixed_rows)
        mixed_wide = mixed_rows.astype(jnp.float32)
        row_scale = lax.rsqrt(jnp.mean(mixed_wide * mixed_wide, axis=-1, keepdims=True) + 1e-05)
        ffn_in = (mixed_wide * row_scale * ffn_gain).astype(jnp.bfloat16)
        flat_routes = routes[0].reshape(-1)
        slot_rank = route_slots(flat_routes)
        position = flat_routes * capp + slot_rank
        token_index = jnp.arange(tokens * TOP, dtype=jnp.int32) // TOP
        source = jnp.zeros((EXPERTS * capp,), jnp.int32).at[position].set(token_index)
        filled = jnp.zeros((EXPERTS * capp,), jnp.bool_).at[position].set(True)
        outgoing = jnp.where(filled[:, None], ffn_in[source], jnp.zeros((), jnp.bfloat16))
        outgoing = outgoing.reshape(EXPERTS * per, chunk, D)
        outgoing, gate_weight, up_weight, down_weight = lax.optimization_barrier(
            (outgoing, gate_weight, up_weight, down_weight)
        )
        per_outer = n_outer // local_experts
        wanted = jnp.arange(n_outer, dtype=jnp.int32) // per_outer

        def collect(weight):
            mine = lax.all_to_all(weight[wanted], "seq_outer", 0, 0, tiled=True)
            return lax.all_gather(mine, "seq_inner", axis=0, tiled=False)

        whole_gate = collect(gate_weight)
        whole_up = collect(up_weight)
        whole_down = collect(down_weight)
        whole_gate = whole_gate.reshape(-1, whole_gate.shape[-1])
        whole_up = whole_up.reshape(-1, whole_up.shape[-1])

        arrived = lax.all_to_all(outgoing, ("ep", "seq_outer", "seq_inner"), 0, 0, tiled=True)
        arrived = arrived.reshape(n_dev * chunk, n_outer, n_inner, D // n_seq)
        arrived = arrived.transpose(0, 2, 1, 3).reshape(n_dev * chunk, D)
        gate_sum = jnp.dot(arrived, whole_gate, preferred_element_type=jnp.float32)
        up_sum = jnp.dot(arrived, whole_up, preferred_element_type=jnp.float32)
        hidden = silu_gate(gate_sum, up_sum).astype(jnp.bfloat16)
        expert_rows = jnp.einsum(
            "rh,xzhd->rzxd", hidden, whole_down, preferred_element_type=jnp.float32
        ).astype(jnp.bfloat16)
        expert_rows = expert_rows.reshape(n_dev, chunk, D)
        returned = lax.all_to_all(expert_rows, ("ep", "seq_outer", "seq_inner"), 0, 0, tiled=True)
        picked = returned.reshape(EXPERTS * capp, D)[position].reshape(tokens, TOP, D)
        expert_mix = jnp.sum(route_gates[0][:, :, None] * picked.astype(jnp.float32), axis=1)
        return (mixed_wide + expert_mix).astype(jnp.bfloat16)[None]

    return shards


def solution(mesh):
    seq = ("seq_outer", "seq_inner")
    placed = (
        P("ep", seq, None),
        P("ep", seq, None),
        P("ep", seq, None),
        P("ep", seq, None),
        P("ep", None, None, None),
        P(),
        P(),
        P("ep", seq, None),
        P("ep", seq, None),
        P("ep", seq, None),
        P("ep", seq, None),
        P("ep", None, seq),
    )
    n_seq, n_ep = mesh.shape["seq"], mesh.shape["ep"]
    n_inner = 2 if n_seq % 2 == 0 else 1
    names = list(mesh.axis_names)
    shape = []
    for name in names:
        shape += [n_seq // n_inner, n_inner] if name == "seq" else [mesh.shape[name]]
    split_names = []
    for name in names:
        split_names += list(seq) if name == "seq" else [name]
    split = Mesh(mesh.devices.reshape(shape), tuple(split_names))
    shards = make_shards(n_ep, n_seq // n_inner, n_inner)
    return jax.shard_map(
        shards, mesh=split, in_specs=placed, out_specs=P("ep", seq, None), check_vma=False
    )
```

```python
import jax
import jax.numpy as jnp
from jax import lax
from jax.sharding import Mesh, PartitionSpec as P

D = 2048
HEADS = 16
HEAD_DIM = 128
EXPERTS = 16
TOP = 6
CAP = 50


def carried_in(array, axis, count):
    total = array
    shift = 1
    while shift < count:
        moved = lax.ppermute(total, axis, [(i, i + shift) for i in range(count - shift)])
        total = total + moved
        shift *= 2
    return total - array


def route_slots(block_routes):
    chosen = (block_routes[:, None] == jnp.arange(EXPERTS, dtype=jnp.int32)[None, :]).astype(
        jnp.int32
    )
    counts = jnp.cumsum(chosen, axis=0) - 1
    return jnp.sum(chosen * counts, axis=1)


def silu_gate(gate_sum, up_sum):
    return gate_sum / (1.0 + jnp.exp(-gate_sum)) * up_sum


def make_shards(n_seq):
    seq = ("seq_hi", "seq_lo")
    group = ("ep", "seq_lo")

    def shards(
        queries,
        key_rows,
        value_rows,
        residual,
        state_start,
        head_gain,
        ffn_gain,
        routes,
        route_gates,
        gate_weight,
        up_weight,
        down_weight,
    ):
        def collect(weight):
            mine = lax.all_to_all(weight, "seq_lo", 0, 0, tiled=False)
            return lax.all_gather(mine, "seq_hi", axis=0, tiled=False)

        whole_gate = collect(gate_weight)
        whole_up = collect(up_weight)
        whole_down = collect(down_weight)
        whole_gate = whole_gate.reshape(-1, whole_gate.shape[-1])
        whole_up = whole_up.reshape(-1, whole_up.shape[-1])

        tokens = queries.shape[1]
        query_heads = queries[0].reshape(tokens, HEADS, HEAD_DIM)
        key_heads = key_rows[0].reshape(tokens, HEADS, HEAD_DIM)
        value_heads = value_rows[0].reshape(tokens, HEADS, HEAD_DIM)
        local_state = jnp.einsum(
            "thd,the->hde", key_heads, value_heads, preferred_element_type=jnp.float32
        )
        earlier = carried_in(local_state, seq, n_seq)
        state_before = state_start[0] + earlier
        causal = (
            jnp.arange(tokens, dtype=jnp.int32)[:, None]
            >= jnp.arange(tokens, dtype=jnp.int32)[None, :]
        )
        scores = jnp.einsum(
            "thd,shd->hts", query_heads, key_heads, preferred_element_type=jnp.float32
        )
        scores = jnp.where(causal[None], scores, 0.0).astype(jnp.bfloat16)
        in_block = jnp.einsum(
            "hts,she->the", scores, value_heads, preferred_element_type=jnp.float32
        )
        from_state = jnp.einsum(
            "thd,hde->the",
            query_heads.astype(jnp.float32),
            state_before,
            precision=lax.Precision.HIGHEST,
        )
        attended = from_state + in_block
        head_scale = lax.rsqrt(jnp.mean(attended * attended, axis=-1, keepdims=True) + 1e-05)
        head_normed = (attended * head_scale).reshape(tokens, D) * head_gain
        mixed_rows = (residual[0].astype(jnp.float32) + head_normed).astype(jnp.bfloat16)
        mixed_rows = lax.optimization_barrier(mixed_rows)
        mixed_wide = mixed_rows.astype(jnp.float32)
        row_scale = lax.rsqrt(jnp.mean(mixed_wide * mixed_wide, axis=-1, keepdims=True) + 1e-05)
        ffn_in = (mixed_wide * row_scale * ffn_gain).astype(jnp.bfloat16)
        flat_routes = routes[0].reshape(-1)
        slot_rank = route_slots(flat_routes)
        position = flat_routes * CAP + slot_rank
        token_index = jnp.arange(tokens * TOP, dtype=jnp.int32) // TOP
        source = jnp.zeros((EXPERTS * CAP,), jnp.int32).at[position].set(token_index)
        filled = jnp.zeros((EXPERTS * CAP,), jnp.bool_).at[position].set(True)
        outgoing = jnp.where(filled[:, None], ffn_in[source], jnp.zeros((), jnp.bfloat16))
        outgoing = outgoing.reshape(EXPERTS, CAP, D)
        arrived = lax.all_to_all(outgoing, group, 0, 0, tiled=True)
        arrived = arrived.reshape(EXPERTS * CAP, D)
        gate_sum = jnp.dot(arrived, whole_gate, preferred_element_type=jnp.float32)
        up_sum = jnp.dot(arrived, whole_up, preferred_element_type=jnp.float32)
        hidden = silu_gate(gate_sum, up_sum).astype(jnp.bfloat16)
        expert_rows = jnp.einsum(
            "rh,abhd->rabd", hidden, whole_down, preferred_element_type=jnp.float32
        ).astype(jnp.bfloat16)
        expert_rows = expert_rows.reshape(EXPERTS, CAP, D)
        returned = lax.all_to_all(expert_rows, group, 0, 0, tiled=True)
        picked = returned.reshape(EXPERTS * CAP, D)[position].reshape(tokens, TOP, D)
        expert_mix = jnp.sum(route_gates[0][:, :, None] * picked.astype(jnp.float32), axis=1)
        return (mixed_wide + expert_mix).astype(jnp.bfloat16)[None]

    return shards


def solution(mesh):
    seq = ("seq_hi", "seq_lo")
    placed = (
        P("ep", seq, None),
        P("ep", seq, None),
        P("ep", seq, None),
        P("ep", seq, None),
        P("ep", None, None, None),
        P(),
        P(),
        P("ep", seq, None),
        P("ep", seq, None),
        P("ep", seq, None),
        P("ep", seq, None),
        P("ep", None, seq),
    )
    n_seq, n_ep = mesh.shape["seq"], mesh.shape["ep"]
    n_lo = EXPERTS // n_ep
    names = list(mesh.axis_names)
    shape, split_names = [], []
    for name in names:
        shape += [n_seq // n_lo, n_lo] if name == "seq" else [mesh.shape[name]]
        split_names += list(seq) if name == "seq" else [name]
    split = Mesh(mesh.devices.reshape(shape), tuple(split_names))
    return jax.shard_map(
        make_shards(n_seq), mesh=split, in_specs=placed, out_specs=P("ep", seq, None),
        check_vma=False,
    )
```

```python
import jax
import jax.numpy as jnp
from jax import lax
from jax.sharding import Mesh, PartitionSpec as P

D = 2048
HEADS = 16
HEAD_DIM = 128
EXPERTS = 16
TOP = 6
CAP = 50


def scanned(array, axis, count):
    total = array
    shift = 1
    while shift < count:
        moved = lax.ppermute(total, axis, [(i, i + shift) for i in range(count - shift)])
        total = total + moved
        shift *= 2
    return total


def summed(array, axis, count):
    total = array
    shift = 1
    while shift < count:
        total = total + lax.ppermute(total, axis, [(i, i ^ shift) for i in range(count)])
        shift *= 2
    return total


def carried_in(array, n_hi, n_lo):
    within = scanned(array, "seq_lo", n_lo) - array
    group_total = summed(array, "seq_lo", n_lo)
    before = scanned(group_total, "seq_hi", n_hi) - group_total
    return within + before


def route_slots(block_routes):
    chosen = (block_routes[:, None] == jnp.arange(EXPERTS, dtype=jnp.int32)[None, :]).astype(
        jnp.int32
    )
    counts = jnp.cumsum(chosen, axis=0) - 1
    return jnp.sum(chosen * counts, axis=1)


def silu_gate(gate_sum, up_sum):
    return gate_sum / (1.0 + jnp.exp(-gate_sum)) * up_sum


def make_shards(n_seq, n_lo):
    seq = ("seq_hi", "seq_lo")
    group = ("ep", "seq_lo")

    def shards(
        queries,
        key_rows,
        value_rows,
        residual,
        state_start,
        head_gain,
        ffn_gain,
        routes,
        route_gates,
        gate_weight,
        up_weight,
        down_weight,
    ):
        def collect(weight):
            across = lax.all_gather(weight, "seq_hi", axis=0, tiled=False)
            return lax.all_to_all(across, "seq_lo", 1, 1, tiled=False)

        whole_gate = collect(gate_weight)
        whole_up = collect(up_weight)
        whole_down = collect(down_weight)
        whole_gate = whole_gate.reshape(-1, whole_gate.shape[-1])
        whole_up = whole_up.reshape(-1, whole_up.shape[-1])

        tokens = queries.shape[1]
        query_heads = queries[0].reshape(tokens, HEADS, HEAD_DIM)
        key_heads = key_rows[0].reshape(tokens, HEADS, HEAD_DIM)
        value_heads = value_rows[0].reshape(tokens, HEADS, HEAD_DIM)
        local_state = jnp.einsum(
            "thd,the->hde", key_heads, value_heads, preferred_element_type=jnp.float32
        )
        earlier = carried_in(local_state, n_seq // n_lo, n_lo)
        state_before = state_start[0] + earlier
        causal = (
            jnp.arange(tokens, dtype=jnp.int32)[:, None]
            >= jnp.arange(tokens, dtype=jnp.int32)[None, :]
        )
        scores = jnp.einsum(
            "thd,shd->hts", query_heads, key_heads, preferred_element_type=jnp.float32
        )
        scores = jnp.where(causal[None], scores, 0.0).astype(jnp.bfloat16)
        in_block = jnp.einsum(
            "hts,she->the", scores, value_heads, preferred_element_type=jnp.float32
        )
        from_state = jnp.einsum(
            "thd,hde->the",
            query_heads.astype(jnp.float32),
            state_before,
            precision=lax.Precision.HIGHEST,
        )
        attended = from_state + in_block
        head_scale = lax.rsqrt(jnp.mean(attended * attended, axis=-1, keepdims=True) + 1e-05)
        head_normed = (attended * head_scale).reshape(tokens, D) * head_gain
        mixed_rows = (residual[0].astype(jnp.float32) + head_normed).astype(jnp.bfloat16)
        mixed_rows = lax.optimization_barrier(mixed_rows)
        mixed_wide = mixed_rows.astype(jnp.float32)
        row_scale = lax.rsqrt(jnp.mean(mixed_wide * mixed_wide, axis=-1, keepdims=True) + 1e-05)
        ffn_in = (mixed_wide * row_scale * ffn_gain).astype(jnp.bfloat16)
        flat_routes = routes[0].reshape(-1)
        slot_rank = route_slots(flat_routes)
        position = flat_routes * CAP + slot_rank
        token_index = jnp.arange(tokens * TOP, dtype=jnp.int32) // TOP
        source = jnp.zeros((EXPERTS * CAP,), jnp.int32).at[position].set(token_index)
        filled = jnp.zeros((EXPERTS * CAP,), jnp.bool_).at[position].set(True)
        outgoing = jnp.where(filled[:, None], ffn_in[source], jnp.zeros((), jnp.bfloat16))
        outgoing = outgoing.reshape(EXPERTS, CAP, D)
        arrived = lax.all_to_all(outgoing, group, 0, 0, tiled=True)
        arrived = arrived.reshape(EXPERTS * CAP, D)
        gate_sum = jnp.dot(arrived, whole_gate, preferred_element_type=jnp.float32)
        up_sum = jnp.dot(arrived, whole_up, preferred_element_type=jnp.float32)
        hidden = silu_gate(gate_sum, up_sum).astype(jnp.bfloat16)
        expert_rows = jnp.einsum(
            "rh,abhd->rabd", hidden, whole_down, preferred_element_type=jnp.float32
        ).astype(jnp.bfloat16)
        expert_rows = expert_rows.reshape(EXPERTS, CAP, D)
        returned = lax.all_to_all(expert_rows, group, 0, 0, tiled=True)
        picked = returned.reshape(EXPERTS * CAP, D)[position].reshape(tokens, TOP, D)
        expert_mix = jnp.sum(route_gates[0][:, :, None] * picked.astype(jnp.float32), axis=1)
        return (mixed_wide + expert_mix).astype(jnp.bfloat16)[None]

    return shards


def solution(mesh):
    seq = ("seq_hi", "seq_lo")
    placed = (
        P("ep", seq, None),
        P("ep", seq, None),
        P("ep", seq, None),
        P("ep", seq, None),
        P("ep", None, None, None),
        P(),
        P(),
        P("ep", seq, None),
        P("ep", seq, None),
        P("ep", seq, None),
        P("ep", seq, None),
        P("ep", None, seq),
    )
    n_seq, n_ep = mesh.shape["seq"], mesh.shape["ep"]
    n_lo = EXPERTS // n_ep
    names = list(mesh.axis_names)
    shape, split_names = [], []
    for name in names:
        shape += [n_seq // n_lo, n_lo] if name == "seq" else [mesh.shape[name]]
        split_names += list(seq) if name == "seq" else [name]
    split = Mesh(mesh.devices.reshape(shape), tuple(split_names))
    return jax.shard_map(
        make_shards(n_seq, n_lo), mesh=split, in_specs=placed, out_specs=P("ep", seq, None),
        check_vma=False,
    )
```

```python
import jax
import jax.numpy as jnp
from jax import lax
from jax.sharding import Mesh, PartitionSpec as P

D = 2048
HEADS = 16
HEAD_DIM = 128
EXPERTS = 16
TOP = 6
CAP = 50


def scanned(array, axis, count):
    total = array
    shift = 1
    while shift < count:
        moved = lax.ppermute(total, axis, [(i, i + shift) for i in range(count - shift)])
        total = total + moved
        shift *= 2
    return total


def summed(array, axis, count):
    total = array
    shift = 1
    while shift < count:
        total = total + lax.ppermute(total, axis, [(i, i ^ shift) for i in range(count)])
        shift *= 2
    return total


def carried_in(array, n_hi, n_lo):
    within = scanned(array, "seq_lo", n_lo) - array
    group_total = summed(array, "seq_lo", n_lo)
    before = scanned(group_total, "seq_hi", n_hi) - group_total
    return within + before


def route_slots(block_routes):
    chosen = (block_routes[:, None] == jnp.arange(EXPERTS, dtype=jnp.int32)[None, :]).astype(
        jnp.int32
    )
    counts = jnp.cumsum(chosen, axis=0) - 1
    return jnp.sum(chosen * counts, axis=1)


def silu_gate(gate_sum, up_sum):
    return gate_sum / (1.0 + jnp.exp(-gate_sum)) * up_sum


def make_shards(n_seq, n_lo):
    seq = ("seq_hi", "seq_lo")
    group = ("ep", "seq_lo")

    def shards(
        queries,
        key_rows,
        value_rows,
        residual,
        state_start,
        head_gain,
        ffn_gain,
        routes,
        route_gates,
        gate_weight,
        up_weight,
        down_weight,
    ):
        mine = [
            lax.all_to_all(weight, "seq_lo", 0, 0, tiled=False)
            for weight in (gate_weight, up_weight, down_weight)
        ]
        *mine, key_rows = lax.optimization_barrier((*mine, key_rows))
        whole_gate, whole_up, whole_down = [
            lax.all_gather(part, "seq_hi", axis=0, tiled=False) for part in mine
        ]
        whole_gate, key_rows, value_rows = lax.optimization_barrier(
            (whole_gate, key_rows, value_rows)
        )
        whole_gate = whole_gate.reshape(-1, whole_gate.shape[-1])
        whole_up = whole_up.reshape(-1, whole_up.shape[-1])

        tokens = queries.shape[1]
        query_heads = queries[0].reshape(tokens, HEADS, HEAD_DIM)
        key_heads = key_rows[0].reshape(tokens, HEADS, HEAD_DIM)
        value_heads = value_rows[0].reshape(tokens, HEADS, HEAD_DIM)
        local_state = jnp.einsum(
            "thd,the->hde", key_heads, value_heads, preferred_element_type=jnp.float32
        )
        earlier = carried_in(local_state, n_seq // n_lo, n_lo)
        state_before = state_start[0] + earlier
        causal = (
            jnp.arange(tokens, dtype=jnp.int32)[:, None]
            >= jnp.arange(tokens, dtype=jnp.int32)[None, :]
        )
        scores = jnp.einsum(
            "thd,shd->hts", query_heads, key_heads, preferred_element_type=jnp.float32
        )
        scores = jnp.where(causal[None], scores, 0.0).astype(jnp.bfloat16)
        in_block = jnp.einsum(
            "hts,she->the", scores, value_heads, preferred_element_type=jnp.float32
        )
        from_state = jnp.einsum(
            "thd,hde->the",
            query_heads.astype(jnp.float32),
            state_before,
            precision=lax.Precision.HIGHEST,
        )
        attended = from_state + in_block
        head_scale = lax.rsqrt(jnp.mean(attended * attended, axis=-1, keepdims=True) + 1e-05)
        head_normed = (attended * head_scale).reshape(tokens, D) * head_gain
        mixed_rows = (residual[0].astype(jnp.float32) + head_normed).astype(jnp.bfloat16)
        mixed_rows = lax.optimization_barrier(mixed_rows)
        mixed_wide = mixed_rows.astype(jnp.float32)
        row_scale = lax.rsqrt(jnp.mean(mixed_wide * mixed_wide, axis=-1, keepdims=True) + 1e-05)
        ffn_in = (mixed_wide * row_scale * ffn_gain).astype(jnp.bfloat16)
        flat_routes = routes[0].reshape(-1)
        slot_rank = route_slots(flat_routes)
        position = flat_routes * CAP + slot_rank
        token_index = jnp.arange(tokens * TOP, dtype=jnp.int32) // TOP
        source = jnp.zeros((EXPERTS * CAP,), jnp.int32).at[position].set(token_index)
        filled = jnp.zeros((EXPERTS * CAP,), jnp.bool_).at[position].set(True)
        outgoing = jnp.where(filled[:, None], ffn_in[source], jnp.zeros((), jnp.bfloat16))
        outgoing = outgoing.reshape(EXPERTS, CAP, D)
        outgoing, whole_up, whole_down = lax.optimization_barrier(
            (outgoing, whole_up, whole_down)
        )
        arrived = lax.all_to_all(outgoing, group, 0, 0, tiled=True)
        arrived = arrived.reshape(EXPERTS * CAP, D)
        gate_sum = jnp.dot(arrived, whole_gate, preferred_element_type=jnp.float32)
        up_sum = jnp.dot(arrived, whole_up, preferred_element_type=jnp.float32)
        hidden = silu_gate(gate_sum, up_sum).astype(jnp.bfloat16)
        expert_rows = jnp.einsum(
            "rh,abhd->rabd", hidden, whole_down, preferred_element_type=jnp.float32
        ).astype(jnp.bfloat16)
        expert_rows = expert_rows.reshape(EXPERTS, CAP, D)
        returned = lax.all_to_all(expert_rows, group, 0, 0, tiled=True)
        picked = returned.reshape(EXPERTS * CAP, D)[position].reshape(tokens, TOP, D)
        expert_mix = jnp.sum(route_gates[0][:, :, None] * picked.astype(jnp.float32), axis=1)
        return (mixed_wide + expert_mix).astype(jnp.bfloat16)[None]

    return shards


def solution(mesh):
    seq = ("seq_hi", "seq_lo")
    placed = (
        P("ep", seq, None),
        P("ep", seq, None),
        P("ep", seq, None),
        P("ep", seq, None),
        P("ep", None, None, None),
        P(),
        P(),
        P("ep", seq, None),
        P("ep", seq, None),
        P("ep", seq, None),
        P("ep", seq, None),
        P("ep", None, seq),
    )
    n_seq, n_ep = mesh.shape["seq"], mesh.shape["ep"]
    n_lo = EXPERTS // n_ep
    names = list(mesh.axis_names)
    shape, split_names = [], []
    for name in names:
        shape += [n_seq // n_lo, n_lo] if name == "seq" else [mesh.shape[name]]
        split_names += list(seq) if name == "seq" else [name]
    split = Mesh(mesh.devices.reshape(shape), tuple(split_names))
    return jax.shard_map(
        make_shards(n_seq, n_lo), mesh=split, in_specs=placed, out_specs=P("ep", seq, None),
        check_vma=False,
    )
```

```python
import jax
import jax.numpy as jnp
from jax import lax
from jax.sharding import Mesh, PartitionSpec as P

D = 2048
HEADS = 16
HEAD_DIM = 128
EXPERTS = 16
TOP = 6
CAP = 50


def carried_in(array, axis, count):
    total = array
    shift = 1
    while shift < count:
        moved = lax.ppermute(total, axis, [(i, i + shift) for i in range(count - shift)])
        total = total + moved
        shift *= 2
    return total - array


def route_slots(block_routes):
    chosen = (block_routes[:, None] == jnp.arange(EXPERTS, dtype=jnp.int32)[None, :]).astype(
        jnp.int32
    )
    counts = jnp.cumsum(chosen, axis=0) - 1
    return jnp.sum(chosen * counts, axis=1)


def silu_gate(gate_sum, up_sum):
    return gate_sum / (1.0 + jnp.exp(-gate_sum)) * up_sum


def make_shards(n_seq):
    seq = ("seq_hi", "seq_lo")
    group = ("ep", "seq_lo")

    def shards(
        queries,
        key_rows,
        value_rows,
        residual,
        state_start,
        head_gain,
        ffn_gain,
        routes,
        route_gates,
        gate_weight,
        up_weight,
        down_weight,
    ):
        slice_rows = gate_weight.shape[1]
        packed = jnp.concatenate(
            [gate_weight, up_weight, jnp.swapaxes(down_weight, 1, 2)], axis=1
        )
        packed = lax.all_to_all(packed, "seq_lo", 0, 0, tiled=False)
        packed = lax.all_gather(packed, "seq_hi", axis=0, tiled=False)
        whole_gate = packed[:, :, :slice_rows]
        whole_up = packed[:, :, slice_rows : 2 * slice_rows]
        whole_down = packed[:, :, 2 * slice_rows :]

        tokens = queries.shape[1]
        query_heads = queries[0].reshape(tokens, HEADS, HEAD_DIM)
        key_heads = key_rows[0].reshape(tokens, HEADS, HEAD_DIM)
        value_heads = value_rows[0].reshape(tokens, HEADS, HEAD_DIM)
        local_state = jnp.einsum(
            "thd,the->hde", key_heads, value_heads, preferred_element_type=jnp.float32
        )
        earlier = carried_in(local_state, seq, n_seq)
        state_before = state_start[0] + earlier
        causal = (
            jnp.arange(tokens, dtype=jnp.int32)[:, None]
            >= jnp.arange(tokens, dtype=jnp.int32)[None, :]
        )
        scores = jnp.einsum(
            "thd,shd->hts", query_heads, key_heads, preferred_element_type=jnp.float32
        )
        scores = jnp.where(causal[None], scores, 0.0).astype(jnp.bfloat16)
        in_block = jnp.einsum(
            "hts,she->the", scores, value_heads, preferred_element_type=jnp.float32
        )
        from_state = jnp.einsum(
            "thd,hde->the",
            query_heads.astype(jnp.float32),
            state_before,
            precision=lax.Precision.HIGHEST,
        )
        attended = from_state + in_block
        head_scale = lax.rsqrt(jnp.mean(attended * attended, axis=-1, keepdims=True) + 1e-05)
        head_normed = (attended * head_scale).reshape(tokens, D) * head_gain
        mixed_rows = (residual[0].astype(jnp.float32) + head_normed).astype(jnp.bfloat16)
        mixed_rows = lax.optimization_barrier(mixed_rows)
        mixed_wide = mixed_rows.astype(jnp.float32)
        row_scale = lax.rsqrt(jnp.mean(mixed_wide * mixed_wide, axis=-1, keepdims=True) + 1e-05)
        ffn_in = (mixed_wide * row_scale * ffn_gain).astype(jnp.bfloat16)
        flat_routes = routes[0].reshape(-1)
        slot_rank = route_slots(flat_routes)
        position = flat_routes * CAP + slot_rank
        token_index = jnp.arange(tokens * TOP, dtype=jnp.int32) // TOP
        source = jnp.zeros((EXPERTS * CAP,), jnp.int32).at[position].set(token_index)
        filled = jnp.zeros((EXPERTS * CAP,), jnp.bool_).at[position].set(True)
        outgoing = jnp.where(filled[:, None], ffn_in[source], jnp.zeros((), jnp.bfloat16))
        outgoing = outgoing.reshape(EXPERTS, CAP, D)
        arrived = lax.all_to_all(outgoing, group, 0, 0, tiled=True)
        arrived = arrived.reshape(EXPERTS * CAP, *whole_gate.shape[:3])
        gate_sum = jnp.einsum(
            "rabd,abdh->rh", arrived, whole_gate, preferred_element_type=jnp.float32
        )
        up_sum = jnp.einsum(
            "rabd,abdh->rh", arrived, whole_up, preferred_element_type=jnp.float32
        )
        hidden = silu_gate(gate_sum, up_sum).astype(jnp.bfloat16)
        expert_rows = jnp.einsum(
            "rh,abdh->rabd", hidden, whole_down, preferred_element_type=jnp.float32
        ).astype(jnp.bfloat16)
        expert_rows = expert_rows.reshape(EXPERTS, CAP, D)
        returned = lax.all_to_all(expert_rows, group, 0, 0, tiled=True)
        picked = returned.reshape(EXPERTS * CAP, D)[position].reshape(tokens, TOP, D)
        expert_mix = jnp.sum(route_gates[0][:, :, None] * picked.astype(jnp.float32), axis=1)
        return (mixed_wide + expert_mix).astype(jnp.bfloat16)[None]

    return shards


def solution(mesh):
    seq = ("seq_hi", "seq_lo")
    placed = (
        P("ep", seq, None),
        P("ep", seq, None),
        P("ep", seq, None),
        P("ep", seq, None),
        P("ep", None, None, None),
        P(),
        P(),
        P("ep", seq, None),
        P("ep", seq, None),
        P("ep", seq, None),
        P("ep", seq, None),
        P("ep", None, seq),
    )
    n_seq, n_ep = mesh.shape["seq"], mesh.shape["ep"]
    n_lo = EXPERTS // n_ep
    names = list(mesh.axis_names)
    shape, split_names = [], []
    for name in names:
        shape += [n_seq // n_lo, n_lo] if name == "seq" else [mesh.shape[name]]
        split_names += list(seq) if name == "seq" else [name]
    split = Mesh(mesh.devices.reshape(shape), tuple(split_names))
    return jax.shard_map(
        make_shards(n_seq), mesh=split, in_specs=placed, out_specs=P("ep", seq, None),
        check_vma=False,
    )
```

```python
import jax
import jax.numpy as jnp
from jax import lax
from jax.sharding import Mesh, PartitionSpec as P

D = 2048
HEADS = 16
HEAD_DIM = 128
EXPERTS = 16
TOP = 6
CAP = 50


def carried_in(array, axis, count):
    total = array
    shift = 1
    while shift < count:
        moved = lax.ppermute(total, axis, [(i, i + shift) for i in range(count - shift)])
        total = total + moved
        shift *= 2
    return total - array


def route_slots(block_routes):
    chosen = (block_routes[:, None] == jnp.arange(EXPERTS, dtype=jnp.int32)[None, :]).astype(
        jnp.int32
    )
    counts = jnp.cumsum(chosen, axis=0) - 1
    return jnp.sum(chosen * counts, axis=1)


def silu_gate(gate_sum, up_sum):
    return gate_sum / (1.0 + jnp.exp(-gate_sum)) * up_sum


def make_shards(n_seq):
    seq = ("seq_hi", "seq_lo")
    group = ("ep", "seq_lo")

    def shards(
        queries,
        key_rows,
        value_rows,
        residual,
        state_start,
        head_gain,
        ffn_gain,
        routes,
        route_gates,
        gate_weight,
        up_weight,
        down_weight,
    ):
        slice_rows = gate_weight.shape[1]
        packed = jnp.concatenate(
            [gate_weight, up_weight, jnp.swapaxes(down_weight, 1, 2)], axis=1
        )
        packed = lax.all_to_all(packed, "seq_lo", 0, 0, tiled=False)
        packed, key_rows, value_rows = lax.optimization_barrier((packed, key_rows, value_rows))
        packed = lax.all_gather(packed, "seq_hi", axis=0, tiled=False)
        whole_gate = packed[:, :, :slice_rows]
        whole_up = packed[:, :, slice_rows : 2 * slice_rows]
        whole_down = packed[:, :, 2 * slice_rows :]

        tokens = queries.shape[1]
        query_heads = queries[0].reshape(tokens, HEADS, HEAD_DIM)
        key_heads = key_rows[0].reshape(tokens, HEADS, HEAD_DIM)
        value_heads = value_rows[0].reshape(tokens, HEADS, HEAD_DIM)
        local_state = jnp.einsum(
            "thd,the->hde", key_heads, value_heads, preferred_element_type=jnp.float32
        )
        earlier = carried_in(local_state, seq, n_seq)
        state_before = state_start[0] + earlier
        causal = (
            jnp.arange(tokens, dtype=jnp.int32)[:, None]
            >= jnp.arange(tokens, dtype=jnp.int32)[None, :]
        )
        scores = jnp.einsum(
            "thd,shd->hts", query_heads, key_heads, preferred_element_type=jnp.float32
        )
        scores = jnp.where(causal[None], scores, 0.0).astype(jnp.bfloat16)
        in_block = jnp.einsum(
            "hts,she->the", scores, value_heads, preferred_element_type=jnp.float32
        )
        from_state = jnp.einsum(
            "thd,hde->the",
            query_heads.astype(jnp.float32),
            state_before,
            precision=lax.Precision.HIGHEST,
        )
        attended = from_state + in_block
        head_scale = lax.rsqrt(jnp.mean(attended * attended, axis=-1, keepdims=True) + 1e-05)
        head_normed = (attended * head_scale).reshape(tokens, D) * head_gain
        mixed_rows = (residual[0].astype(jnp.float32) + head_normed).astype(jnp.bfloat16)
        mixed_rows = lax.optimization_barrier(mixed_rows)
        mixed_wide = mixed_rows.astype(jnp.float32)
        row_scale = lax.rsqrt(jnp.mean(mixed_wide * mixed_wide, axis=-1, keepdims=True) + 1e-05)
        ffn_in = (mixed_wide * row_scale * ffn_gain).astype(jnp.bfloat16)
        flat_routes = routes[0].reshape(-1)
        slot_rank = route_slots(flat_routes)
        position = flat_routes * CAP + slot_rank
        token_index = jnp.arange(tokens * TOP, dtype=jnp.int32) // TOP
        source = jnp.zeros((EXPERTS * CAP,), jnp.int32).at[position].set(token_index)
        filled = jnp.zeros((EXPERTS * CAP,), jnp.bool_).at[position].set(True)
        outgoing = jnp.where(filled[:, None], ffn_in[source], jnp.zeros((), jnp.bfloat16))
        outgoing = outgoing.reshape(EXPERTS, CAP, D)
        arrived = lax.all_to_all(outgoing, group, 0, 0, tiled=True)
        arrived = arrived.reshape(EXPERTS * CAP, *whole_gate.shape[:3])
        gate_sum = jnp.einsum(
            "rabd,abdh->rh", arrived, whole_gate, preferred_element_type=jnp.float32
        )
        up_sum = jnp.einsum(
            "rabd,abdh->rh", arrived, whole_up, preferred_element_type=jnp.float32
        )
        hidden = silu_gate(gate_sum, up_sum).astype(jnp.bfloat16)
        expert_rows = jnp.einsum(
            "rh,abdh->rabd", hidden, whole_down, preferred_element_type=jnp.float32
        ).astype(jnp.bfloat16)
        expert_rows = expert_rows.reshape(EXPERTS, CAP, D)
        returned = lax.all_to_all(expert_rows, group, 0, 0, tiled=True)
        picked = returned.reshape(EXPERTS * CAP, D)[position].reshape(tokens, TOP, D)
        expert_mix = jnp.sum(route_gates[0][:, :, None] * picked.astype(jnp.float32), axis=1)
        return (mixed_wide + expert_mix).astype(jnp.bfloat16)[None]

    return shards


def solution(mesh):
    seq = ("seq_hi", "seq_lo")
    placed = (
        P("ep", seq, None),
        P("ep", seq, None),
        P("ep", seq, None),
        P("ep", seq, None),
        P("ep", None, None, None),
        P(),
        P(),
        P("ep", seq, None),
        P("ep", seq, None),
        P("ep", seq, None),
        P("ep", seq, None),
        P("ep", None, seq),
    )
    n_seq, n_ep = mesh.shape["seq"], mesh.shape["ep"]
    n_lo = EXPERTS // n_ep
    names = list(mesh.axis_names)
    shape, split_names = [], []
    for name in names:
        shape += [n_seq // n_lo, n_lo] if name == "seq" else [mesh.shape[name]]
        split_names += list(seq) if name == "seq" else [name]
    split = Mesh(mesh.devices.reshape(shape), tuple(split_names))
    return jax.shard_map(
        make_shards(n_seq), mesh=split, in_specs=placed, out_specs=P("ep", seq, None),
        check_vma=False,
    )
```

```python
import jax
import jax.numpy as jnp
from jax import lax
from jax.sharding import Mesh, PartitionSpec as P

D = 2048
HEADS = 16
HEAD_DIM = 128
EXPERTS = 16
TOP = 6
CAP = 50


def carried_in(array, axis, count):
    total = array
    shift = 1
    while shift < count:
        moved = lax.ppermute(total, axis, [(i, i + shift) for i in range(count - shift)])
        total = total + moved
        shift *= 2
    return total - array


def route_slots(block_routes):
    chosen = (block_routes[:, None] == jnp.arange(EXPERTS, dtype=jnp.int32)[None, :]).astype(
        jnp.int32
    )
    counts = jnp.cumsum(chosen, axis=0) - 1
    return jnp.sum(chosen * counts, axis=1)


def silu_gate(gate_sum, up_sum):
    return gate_sum / (1.0 + jnp.exp(-gate_sum)) * up_sum


def make_shards(n_seq):
    seq = ("seq_hi", "seq_lo")
    group = ("ep", "seq_lo")

    def shards(
        queries,
        key_rows,
        value_rows,
        residual,
        state_start,
        head_gain,
        ffn_gain,
        routes,
        route_gates,
        gate_weight,
        up_weight,
        down_weight,
    ):
        tokens = queries.shape[1]
        query_heads = queries[0].reshape(tokens, HEADS, HEAD_DIM)
        key_heads = key_rows[0].reshape(tokens, HEADS, HEAD_DIM)
        value_heads = value_rows[0].reshape(tokens, HEADS, HEAD_DIM)
        local_state = jnp.einsum(
            "thd,the->hde", key_heads, value_heads, preferred_element_type=jnp.float32
        )
        earlier = carried_in(local_state, seq, n_seq)
        earlier, gate_weight, up_weight, down_weight = lax.optimization_barrier(
            (earlier, gate_weight, up_weight, down_weight)
        )
        slice_rows = gate_weight.shape[1]
        packed = jnp.concatenate(
            [gate_weight, up_weight, jnp.swapaxes(down_weight, 1, 2)], axis=1
        )
        packed = lax.all_to_all(packed, "seq_lo", 0, 0, tiled=False)
        packed = lax.all_gather(packed, "seq_hi", axis=0, tiled=False)
        whole_gate = packed[:, :, :slice_rows]
        whole_up = packed[:, :, slice_rows : 2 * slice_rows]
        whole_down = packed[:, :, 2 * slice_rows :]

        state_before = state_start[0] + earlier
        causal = (
            jnp.arange(tokens, dtype=jnp.int32)[:, None]
            >= jnp.arange(tokens, dtype=jnp.int32)[None, :]
        )
        scores = jnp.einsum(
            "thd,shd->hts", query_heads, key_heads, preferred_element_type=jnp.float32
        )
        scores = jnp.where(causal[None], scores, 0.0).astype(jnp.bfloat16)
        in_block = jnp.einsum(
            "hts,she->the", scores, value_heads, preferred_element_type=jnp.float32
        )
        from_state = jnp.einsum(
            "thd,hde->the",
            query_heads.astype(jnp.float32),
            state_before,
            precision=lax.Precision.HIGHEST,
        )
        attended = from_state + in_block
        head_scale = lax.rsqrt(jnp.mean(attended * attended, axis=-1, keepdims=True) + 1e-05)
        head_normed = (attended * head_scale).reshape(tokens, D) * head_gain
        mixed_rows = (residual[0].astype(jnp.float32) + head_normed).astype(jnp.bfloat16)
        mixed_rows = lax.optimization_barrier(mixed_rows)
        mixed_wide = mixed_rows.astype(jnp.float32)
        row_scale = lax.rsqrt(jnp.mean(mixed_wide * mixed_wide, axis=-1, keepdims=True) + 1e-05)
        ffn_in = (mixed_wide * row_scale * ffn_gain).astype(jnp.bfloat16)
        flat_routes = routes[0].reshape(-1)
        slot_rank = route_slots(flat_routes)
        position = flat_routes * CAP + slot_rank
        token_index = jnp.arange(tokens * TOP, dtype=jnp.int32) // TOP
        source = jnp.zeros((EXPERTS * CAP,), jnp.int32).at[position].set(token_index)
        filled = jnp.zeros((EXPERTS * CAP,), jnp.bool_).at[position].set(True)
        outgoing = jnp.where(filled[:, None], ffn_in[source], jnp.zeros((), jnp.bfloat16))
        outgoing = outgoing.reshape(EXPERTS, CAP, D)
        arrived = lax.all_to_all(outgoing, group, 0, 0, tiled=True)
        arrived = arrived.reshape(EXPERTS * CAP, *whole_gate.shape[:3])
        gate_sum = jnp.einsum(
            "rabd,abdh->rh", arrived, whole_gate, preferred_element_type=jnp.float32
        )
        up_sum = jnp.einsum(
            "rabd,abdh->rh", arrived, whole_up, preferred_element_type=jnp.float32
        )
        hidden = silu_gate(gate_sum, up_sum).astype(jnp.bfloat16)
        expert_rows = jnp.einsum(
            "rh,abdh->rabd", hidden, whole_down, preferred_element_type=jnp.float32
        ).astype(jnp.bfloat16)
        expert_rows = expert_rows.reshape(EXPERTS, CAP, D)
        returned = lax.all_to_all(expert_rows, group, 0, 0, tiled=True)
        picked = returned.reshape(EXPERTS * CAP, D)[position].reshape(tokens, TOP, D)
        expert_mix = jnp.sum(route_gates[0][:, :, None] * picked.astype(jnp.float32), axis=1)
        return (mixed_wide + expert_mix).astype(jnp.bfloat16)[None]

    return shards


def solution(mesh):
    seq = ("seq_hi", "seq_lo")
    placed = (
        P("ep", seq, None),
        P("ep", seq, None),
        P("ep", seq, None),
        P("ep", seq, None),
        P("ep", None, None, None),
        P(),
        P(),
        P("ep", seq, None),
        P("ep", seq, None),
        P("ep", seq, None),
        P("ep", seq, None),
        P("ep", None, seq),
    )
    n_seq, n_ep = mesh.shape["seq"], mesh.shape["ep"]
    n_lo = EXPERTS // n_ep
    names = list(mesh.axis_names)
    shape, split_names = [], []
    for name in names:
        shape += [n_seq // n_lo, n_lo] if name == "seq" else [mesh.shape[name]]
        split_names += list(seq) if name == "seq" else [name]
    split = Mesh(mesh.devices.reshape(shape), tuple(split_names))
    return jax.shard_map(
        make_shards(n_seq), mesh=split, in_specs=placed, out_specs=P("ep", seq, None),
        check_vma=False,
    )
```

```python
import jax
import jax.numpy as jnp
from jax import lax
from jax.sharding import Mesh, PartitionSpec as P

D = 2048
HEADS = 16
HEAD_DIM = 128
EXPERTS = 16
TOP = 6
CAP = 50


def carried_in(array, axis, count):
    total = array
    shift = 1
    while shift < count:
        moved = lax.ppermute(total, axis, [(i, i + shift) for i in range(count - shift)])
        total = total + moved
        shift *= 2
    return total - array


def route_slots(block_routes):
    chosen = (block_routes[:, None] == jnp.arange(EXPERTS, dtype=jnp.int32)[None, :]).astype(
        jnp.int32
    )
    counts = jnp.cumsum(chosen, axis=0) - 1
    return jnp.sum(chosen * counts, axis=1)


def silu_gate(gate_sum, up_sum):
    return gate_sum / (1.0 + jnp.exp(-gate_sum)) * up_sum


def make_shards(n_seq):
    seq = ("seq_hi", "seq_lo")
    group = ("ep", "seq_lo")

    def shards(
        queries,
        key_rows,
        value_rows,
        residual,
        state_start,
        head_gain,
        ffn_gain,
        routes,
        route_gates,
        gate_weight,
        up_weight,
        down_weight,
    ):
        slice_rows = gate_weight.shape[1]
        packed = jnp.concatenate(
            [gate_weight, up_weight, jnp.swapaxes(down_weight, 1, 2)], axis=1
        )
        across = lax.all_gather(packed, "seq_hi", axis=0, tiled=False)

        tokens = queries.shape[1]
        query_heads = queries[0].reshape(tokens, HEADS, HEAD_DIM)
        key_heads = key_rows[0].reshape(tokens, HEADS, HEAD_DIM)
        value_heads = value_rows[0].reshape(tokens, HEADS, HEAD_DIM)
        local_state = jnp.einsum(
            "thd,the->hde", key_heads, value_heads, preferred_element_type=jnp.float32
        )
        earlier = carried_in(local_state, seq, n_seq)
        state_before = state_start[0] + earlier
        causal = (
            jnp.arange(tokens, dtype=jnp.int32)[:, None]
            >= jnp.arange(tokens, dtype=jnp.int32)[None, :]
        )
        scores = jnp.einsum(
            "thd,shd->hts", query_heads, key_heads, preferred_element_type=jnp.float32
        )
        scores = jnp.where(causal[None], scores, 0.0).astype(jnp.bfloat16)
        in_block = jnp.einsum(
            "hts,she->the", scores, value_heads, preferred_element_type=jnp.float32
        )
        from_state = jnp.einsum(
            "thd,hde->the",
            query_heads.astype(jnp.float32),
            state_before,
            precision=lax.Precision.HIGHEST,
        )
        attended = from_state + in_block
        head_scale = lax.rsqrt(jnp.mean(attended * attended, axis=-1, keepdims=True) + 1e-05)
        head_normed = (attended * head_scale).reshape(tokens, D) * head_gain
        mixed_rows = (residual[0].astype(jnp.float32) + head_normed).astype(jnp.bfloat16)
        mixed_rows = lax.optimization_barrier(mixed_rows)
        mixed_wide = mixed_rows.astype(jnp.float32)
        row_scale = lax.rsqrt(jnp.mean(mixed_wide * mixed_wide, axis=-1, keepdims=True) + 1e-05)
        ffn_in = (mixed_wide * row_scale * ffn_gain).astype(jnp.bfloat16)
        flat_routes = routes[0].reshape(-1)
        slot_rank = route_slots(flat_routes)
        position = flat_routes * CAP + slot_rank
        token_index = jnp.arange(tokens * TOP, dtype=jnp.int32) // TOP
        source = jnp.zeros((EXPERTS * CAP,), jnp.int32).at[position].set(token_index)
        filled = jnp.zeros((EXPERTS * CAP,), jnp.bool_).at[position].set(True)
        outgoing = jnp.where(filled[:, None], ffn_in[source], jnp.zeros((), jnp.bfloat16))
        outgoing = outgoing.reshape(EXPERTS, CAP, D)
        arrived = lax.all_to_all(outgoing, group, 0, 0, tiled=True)
        across, arrived = lax.optimization_barrier((across, arrived))
        packed = lax.all_to_all(across, "seq_lo", 1, 1, tiled=False)
        whole_gate = packed[:, :, :slice_rows]
        whole_up = packed[:, :, slice_rows : 2 * slice_rows]
        whole_down = packed[:, :, 2 * slice_rows :]
        arrived = arrived.reshape(EXPERTS * CAP, *whole_gate.shape[:3])
        gate_sum = jnp.einsum(
            "rabd,abdh->rh", arrived, whole_gate, preferred_element_type=jnp.float32
        )
        up_sum = jnp.einsum(
            "rabd,abdh->rh", arrived, whole_up, preferred_element_type=jnp.float32
        )
        hidden = silu_gate(gate_sum, up_sum).astype(jnp.bfloat16)
        expert_rows = jnp.einsum(
            "rh,abdh->rabd", hidden, whole_down, preferred_element_type=jnp.float32
        ).astype(jnp.bfloat16)
        expert_rows = expert_rows.reshape(EXPERTS, CAP, D)
        returned = lax.all_to_all(expert_rows, group, 0, 0, tiled=True)
        picked = returned.reshape(EXPERTS * CAP, D)[position].reshape(tokens, TOP, D)
        expert_mix = jnp.sum(route_gates[0][:, :, None] * picked.astype(jnp.float32), axis=1)
        return (mixed_wide + expert_mix).astype(jnp.bfloat16)[None]

    return shards


def solution(mesh):
    seq = ("seq_hi", "seq_lo")
    placed = (
        P("ep", seq, None),
        P("ep", seq, None),
        P("ep", seq, None),
        P("ep", seq, None),
        P("ep", None, None, None),
        P(),
        P(),
        P("ep", seq, None),
        P("ep", seq, None),
        P("ep", seq, None),
        P("ep", seq, None),
        P("ep", None, seq),
    )
    n_seq, n_ep = mesh.shape["seq"], mesh.shape["ep"]
    n_lo = EXPERTS // n_ep
    names = list(mesh.axis_names)
    shape, split_names = [], []
    for name in names:
        shape += [n_seq // n_lo, n_lo] if name == "seq" else [mesh.shape[name]]
        split_names += list(seq) if name == "seq" else [name]
    split = Mesh(mesh.devices.reshape(shape), tuple(split_names))
    return jax.shard_map(
        make_shards(n_seq), mesh=split, in_specs=placed, out_specs=P("ep", seq, None),
        check_vma=False,
    )
```

```python
import jax
import jax.numpy as jnp
from jax import lax
from jax.sharding import Mesh, PartitionSpec as P

D = 2048
HEADS = 16
HEAD_DIM = 128
EXPERTS = 16
TOP = 6
CAP = 50


def carried_in(array, axis, count):
    total = array
    shift = 1
    while shift < count:
        moved = lax.ppermute(total, axis, [(i, i + shift) for i in range(count - shift)])
        total = total + moved
        shift *= 2
    return total - array


def route_slots(block_routes):
    chosen = (block_routes[:, None] == jnp.arange(EXPERTS, dtype=jnp.int32)[None, :]).astype(
        jnp.int32
    )
    counts = jnp.cumsum(chosen, axis=0) - 1
    return jnp.sum(chosen * counts, axis=1)


def silu_gate(gate_sum, up_sum):
    return gate_sum / (1.0 + jnp.exp(-gate_sum)) * up_sum


def make_shards(n_seq):
    seq = ("seq_hi", "seq_lo")
    group = ("ep", "seq_lo")

    def shards(
        queries,
        key_rows,
        value_rows,
        residual,
        state_start,
        head_gain,
        ffn_gain,
        routes,
        route_gates,
        gate_weight,
        up_weight,
        down_weight,
    ):
        tokens = queries.shape[1]
        query_heads = queries[0].reshape(tokens, HEADS, HEAD_DIM)
        key_heads = key_rows[0].reshape(tokens, HEADS, HEAD_DIM)
        value_heads = value_rows[0].reshape(tokens, HEADS, HEAD_DIM)
        local_state = jnp.einsum(
            "thd,the->hde", key_heads, value_heads, preferred_element_type=jnp.float32
        )
        earlier = carried_in(local_state, seq, n_seq)
        earlier, gate_weight, up_weight, down_weight = lax.optimization_barrier(
            (earlier, gate_weight, up_weight, down_weight)
        )
        def collect(weight):
            mine = lax.all_to_all(weight, "seq_lo", 0, 0, tiled=False)
            return lax.all_gather(mine, "seq_hi", axis=0, tiled=False)

        whole_gate = collect(gate_weight)
        whole_up = collect(up_weight)
        whole_down = collect(down_weight)
        whole_gate = whole_gate.reshape(-1, whole_gate.shape[-1])
        whole_up = whole_up.reshape(-1, whole_up.shape[-1])

        state_before = state_start[0] + earlier
        causal = (
            jnp.arange(tokens, dtype=jnp.int32)[:, None]
            >= jnp.arange(tokens, dtype=jnp.int32)[None, :]
        )
        scores = jnp.einsum(
            "thd,shd->hts", query_heads, key_heads, preferred_element_type=jnp.float32
        )
        scores = jnp.where(causal[None], scores, 0.0).astype(jnp.bfloat16)
        in_block = jnp.einsum(
            "hts,she->the", scores, value_heads, preferred_element_type=jnp.float32
        )
        from_state = jnp.einsum(
            "thd,hde->the",
            query_heads.astype(jnp.float32),
            state_before,
            precision=lax.Precision.HIGHEST,
        )
        attended = from_state + in_block
        head_scale = lax.rsqrt(jnp.mean(attended * attended, axis=-1, keepdims=True) + 1e-05)
        head_normed = (attended * head_scale).reshape(tokens, D) * head_gain
        mixed_rows = (residual[0].astype(jnp.float32) + head_normed).astype(jnp.bfloat16)
        mixed_rows = lax.optimization_barrier(mixed_rows)
        mixed_wide = mixed_rows.astype(jnp.float32)
        row_scale = lax.rsqrt(jnp.mean(mixed_wide * mixed_wide, axis=-1, keepdims=True) + 1e-05)
        ffn_in = (mixed_wide * row_scale * ffn_gain).astype(jnp.bfloat16)
        flat_routes = routes[0].reshape(-1)
        slot_rank = route_slots(flat_routes)
        position = flat_routes * CAP + slot_rank
        token_index = jnp.arange(tokens * TOP, dtype=jnp.int32) // TOP
        source = jnp.zeros((EXPERTS * CAP,), jnp.int32).at[position].set(token_index)
        filled = jnp.zeros((EXPERTS * CAP,), jnp.bool_).at[position].set(True)
        outgoing = jnp.where(filled[:, None], ffn_in[source], jnp.zeros((), jnp.bfloat16))
        outgoing = outgoing.reshape(EXPERTS, CAP, D)
        arrived = lax.all_to_all(outgoing, group, 0, 0, tiled=True)
        arrived = arrived.reshape(EXPERTS * CAP, D)
        gate_sum = jnp.dot(arrived, whole_gate, preferred_element_type=jnp.float32)
        up_sum = jnp.dot(arrived, whole_up, preferred_element_type=jnp.float32)
        hidden = silu_gate(gate_sum, up_sum).astype(jnp.bfloat16)
        expert_rows = jnp.einsum(
            "rh,abhd->rabd", hidden, whole_down, preferred_element_type=jnp.float32
        ).astype(jnp.bfloat16)
        expert_rows = expert_rows.reshape(EXPERTS, CAP, D)
        returned = lax.all_to_all(expert_rows, group, 0, 0, tiled=True)
        picked = returned.reshape(EXPERTS * CAP, D)[position].reshape(tokens, TOP, D)
        expert_mix = jnp.sum(route_gates[0][:, :, None] * picked.astype(jnp.float32), axis=1)
        return (mixed_wide + expert_mix).astype(jnp.bfloat16)[None]

    return shards


def solution(mesh):
    seq = ("seq_hi", "seq_lo")
    placed = (
        P("ep", seq, None),
        P("ep", seq, None),
        P("ep", seq, None),
        P("ep", seq, None),
        P("ep", None, None, None),
        P(),
        P(),
        P("ep", seq, None),
        P("ep", seq, None),
        P("ep", seq, None),
        P("ep", seq, None),
        P("ep", None, seq),
    )
    n_seq, n_ep = mesh.shape["seq"], mesh.shape["ep"]
    n_lo = EXPERTS // n_ep
    names = list(mesh.axis_names)
    shape, split_names = [], []
    for name in names:
        shape += [n_seq // n_lo, n_lo] if name == "seq" else [mesh.shape[name]]
        split_names += list(seq) if name == "seq" else [name]
    split = Mesh(mesh.devices.reshape(shape), tuple(split_names))
    return jax.shard_map(
        make_shards(n_seq), mesh=split, in_specs=placed, out_specs=P("ep", seq, None),
        check_vma=False,
    )
```

```python
import jax
import jax.numpy as jnp
from jax import lax
from jax.sharding import Mesh, PartitionSpec as P

D = 2048
HEADS = 16
HEAD_DIM = 128
EXPERTS = 16
TOP = 6
CAP = 50


def carried_in(array, axis, count):
    total = array
    shift = 1
    while shift < count:
        moved = lax.ppermute(total, axis, [(i, i + shift) for i in range(count - shift)])
        total = total + moved
        shift *= 2
    return total - array


def route_slots(block_routes):
    chosen = (block_routes[:, None] == jnp.arange(EXPERTS, dtype=jnp.int32)[None, :]).astype(
        jnp.int32
    )
    counts = jnp.cumsum(chosen, axis=0) - 1
    return jnp.sum(chosen * counts, axis=1)


def silu_gate(gate_sum, up_sum):
    return gate_sum / (1.0 + jnp.exp(-gate_sum)) * up_sum


def make_shards(n_seq):
    seq = ("seq_hi", "seq_lo")
    group = ("ep", "seq_lo")

    def shards(
        queries,
        key_rows,
        value_rows,
        residual,
        state_start,
        head_gain,
        ffn_gain,
        routes,
        route_gates,
        gate_weight,
        up_weight,
        down_weight,
    ):
        def collect(weight):
            mine = lax.all_to_all(weight, "seq_lo", 0, 0, tiled=False)
            return lax.all_gather(mine, "seq_hi", axis=0, tiled=False)

        gate_across = lax.all_gather(gate_weight, "seq_hi", axis=0, tiled=False)
        whole_up = collect(up_weight)
        whole_down = collect(down_weight)
        whole_up = whole_up.reshape(-1, whole_up.shape[-1])

        tokens = queries.shape[1]
        query_heads = queries[0].reshape(tokens, HEADS, HEAD_DIM)
        key_heads = key_rows[0].reshape(tokens, HEADS, HEAD_DIM)
        value_heads = value_rows[0].reshape(tokens, HEADS, HEAD_DIM)
        local_state = jnp.einsum(
            "thd,the->hde", key_heads, value_heads, preferred_element_type=jnp.float32
        )
        earlier = carried_in(local_state, seq, n_seq)
        gate_across, earlier = lax.optimization_barrier((gate_across, earlier))
        whole_gate = lax.all_to_all(gate_across, "seq_lo", 1, 1, tiled=False)
        whole_gate = whole_gate.reshape(-1, whole_gate.shape[-1])
        state_before = state_start[0] + earlier
        causal = (
            jnp.arange(tokens, dtype=jnp.int32)[:, None]
            >= jnp.arange(tokens, dtype=jnp.int32)[None, :]
        )
        scores = jnp.einsum(
            "thd,shd->hts", query_heads, key_heads, preferred_element_type=jnp.float32
        )
        scores = jnp.where(causal[None], scores, 0.0).astype(jnp.bfloat16)
        in_block = jnp.einsum(
            "hts,she->the", scores, value_heads, preferred_element_type=jnp.float32
        )
        from_state = jnp.einsum(
            "thd,hde->the",
            query_heads.astype(jnp.float32),
            state_before,
            precision=lax.Precision.HIGHEST,
        )
        attended = from_state + in_block
        head_scale = lax.rsqrt(jnp.mean(attended * attended, axis=-1, keepdims=True) + 1e-05)
        head_normed = (attended * head_scale).reshape(tokens, D) * head_gain
        mixed_rows = (residual[0].astype(jnp.float32) + head_normed).astype(jnp.bfloat16)
        mixed_rows = lax.optimization_barrier(mixed_rows)
        mixed_wide = mixed_rows.astype(jnp.float32)
        row_scale = lax.rsqrt(jnp.mean(mixed_wide * mixed_wide, axis=-1, keepdims=True) + 1e-05)
        ffn_in = (mixed_wide * row_scale * ffn_gain).astype(jnp.bfloat16)
        flat_routes = routes[0].reshape(-1)
        slot_rank = route_slots(flat_routes)
        position = flat_routes * CAP + slot_rank
        token_index = jnp.arange(tokens * TOP, dtype=jnp.int32) // TOP
        source = jnp.zeros((EXPERTS * CAP,), jnp.int32).at[position].set(token_index)
        filled = jnp.zeros((EXPERTS * CAP,), jnp.bool_).at[position].set(True)
        outgoing = jnp.where(filled[:, None], ffn_in[source], jnp.zeros((), jnp.bfloat16))
        outgoing = outgoing.reshape(EXPERTS, CAP, D)
        outgoing, whole_up, whole_down = lax.optimization_barrier(
            (outgoing, whole_up, whole_down)
        )
        arrived = lax.all_to_all(outgoing, group, 0, 0, tiled=True)
        arrived = arrived.reshape(EXPERTS * CAP, D)
        gate_sum = jnp.dot(arrived, whole_gate, preferred_element_type=jnp.float32)
        up_sum = jnp.dot(arrived, whole_up, preferred_element_type=jnp.float32)
        hidden = silu_gate(gate_sum, up_sum).astype(jnp.bfloat16)
        expert_rows = jnp.einsum(
            "rh,abhd->rabd", hidden, whole_down, preferred_element_type=jnp.float32
        ).astype(jnp.bfloat16)
        expert_rows = expert_rows.reshape(EXPERTS, CAP, D)
        returned = lax.all_to_all(expert_rows, group, 0, 0, tiled=True)
        picked = returned.reshape(EXPERTS * CAP, D)[position].reshape(tokens, TOP, D)
        expert_mix = jnp.sum(route_gates[0][:, :, None] * picked.astype(jnp.float32), axis=1)
        return (mixed_wide + expert_mix).astype(jnp.bfloat16)[None]

    return shards


def solution(mesh):
    seq = ("seq_hi", "seq_lo")
    placed = (
        P("ep", seq, None),
        P("ep", seq, None),
        P("ep", seq, None),
        P("ep", seq, None),
        P("ep", None, None, None),
        P(),
        P(),
        P("ep", seq, None),
        P("ep", seq, None),
        P("ep", seq, None),
        P("ep", seq, None),
        P("ep", None, seq),
    )
    n_seq, n_ep = mesh.shape["seq"], mesh.shape["ep"]
    n_lo = EXPERTS // n_ep
    names = list(mesh.axis_names)
    shape, split_names = [], []
    for name in names:
        shape += [n_seq // n_lo, n_lo] if name == "seq" else [mesh.shape[name]]
        split_names += list(seq) if name == "seq" else [name]
    split = Mesh(mesh.devices.reshape(shape), tuple(split_names))
    return jax.shard_map(
        make_shards(n_seq), mesh=split, in_specs=placed, out_specs=P("ep", seq, None),
        check_vma=False,
    )
```

```python
import jax
import jax.numpy as jnp
from jax import lax
from jax.sharding import Mesh, PartitionSpec as P

D = 2048
HEADS = 16
HEAD_DIM = 128
EXPERTS = 16
TOP = 6
CAP = 50


def carried_in(array, axis, count):
    total = array
    shift = 1
    while shift < count:
        moved = lax.ppermute(total, axis, [(i, i + shift) for i in range(count - shift)])
        total = total + moved
        shift *= 2
    return total - array


def route_slots(block_routes):
    chosen = (block_routes[:, None] == jnp.arange(EXPERTS, dtype=jnp.int32)[None, :]).astype(
        jnp.int32
    )
    counts = jnp.cumsum(chosen, axis=0) - 1
    return jnp.sum(chosen * counts, axis=1)


def silu_gate(gate_sum, up_sum):
    return gate_sum / (1.0 + jnp.exp(-gate_sum)) * up_sum


def make_shards(n_seq):
    seq = ("seq_hi", "seq_lo")
    group = ("ep", "seq_lo")

    def shards(
        queries,
        key_rows,
        value_rows,
        residual,
        state_start,
        head_gain,
        ffn_gain,
        routes,
        route_gates,
        gate_weight,
        up_weight,
        down_weight,
    ):
        def collect(weight):
            mine = lax.all_to_all(weight, "seq_lo", 0, 0, tiled=False)
            return lax.all_gather(mine, "seq_hi", axis=0, tiled=False)

        whole_gate = collect(gate_weight)
        whole_up = collect(up_weight)
        whole_down = collect(down_weight)
        whole_gate = whole_gate.reshape(-1, whole_gate.shape[-1])
        whole_up = whole_up.reshape(-1, whole_up.shape[-1])

        tokens = queries.shape[1]
        query_heads = queries[0].reshape(tokens, HEADS, HEAD_DIM)
        key_heads = key_rows[0].reshape(tokens, HEADS, HEAD_DIM)
        value_heads = value_rows[0].reshape(tokens, HEADS, HEAD_DIM)
        local_state = jnp.einsum(
            "thd,the->hde", key_heads, value_heads, preferred_element_type=jnp.float32
        )
        earlier = carried_in(local_state, seq, n_seq)
        state_before = state_start[0] + earlier
        causal = (
            jnp.arange(tokens, dtype=jnp.int32)[:, None]
            >= jnp.arange(tokens, dtype=jnp.int32)[None, :]
        )
        scores = jnp.einsum(
            "thd,shd->hts", query_heads, key_heads, preferred_element_type=jnp.float32
        )
        scores = jnp.where(causal[None], scores, 0.0).astype(jnp.bfloat16)
        in_block = jnp.einsum(
            "hts,she->the", scores, value_heads, preferred_element_type=jnp.float32
        )
        from_state = jnp.einsum(
            "thd,hde->the",
            query_heads.astype(jnp.float32),
            state_before,
            precision=lax.Precision.HIGHEST,
        )
        attended = from_state + in_block
        head_scale = lax.rsqrt(jnp.mean(attended * attended, axis=-1, keepdims=True) + 1e-05)
        head_normed = (attended * head_scale).reshape(tokens, D) * head_gain
        mixed_rows = (residual[0].astype(jnp.float32) + head_normed).astype(jnp.bfloat16)
        mixed_rows = lax.optimization_barrier(mixed_rows)
        mixed_wide = mixed_rows.astype(jnp.float32)
        row_scale = lax.rsqrt(jnp.mean(mixed_wide * mixed_wide, axis=-1, keepdims=True) + 1e-05)
        ffn_in = (mixed_wide * row_scale * ffn_gain).astype(jnp.bfloat16)
        flat_routes = routes[0].reshape(-1)
        slot_rank = route_slots(flat_routes)
        position = flat_routes * CAP + slot_rank
        token_index = jnp.arange(tokens * TOP, dtype=jnp.int32) // TOP
        source = jnp.zeros((EXPERTS * CAP,), jnp.int32).at[position].set(token_index)
        filled = jnp.zeros((EXPERTS * CAP,), jnp.bool_).at[position].set(True)
        outgoing = jnp.where(filled[:, None], ffn_in[source], jnp.zeros((), jnp.bfloat16))
        outgoing = outgoing.reshape(EXPERTS, CAP, D)
        arrived = lax.all_to_all(outgoing, group, 0, 0, tiled=True)
        arrived = arrived.reshape(EXPERTS * CAP, D)
        gate_sum = jnp.dot(arrived, whole_gate, preferred_element_type=jnp.float32)
        up_sum = jnp.dot(arrived, whole_up, preferred_element_type=jnp.float32)
        hidden = silu_gate(gate_sum, up_sum).astype(jnp.bfloat16)
        expert_rows = jnp.einsum(
            "rh,abhd->rabd", hidden, whole_down, preferred_element_type=jnp.float32
        ).astype(jnp.bfloat16)
        expert_rows = expert_rows.reshape(EXPERTS, CAP, D)
        returned = lax.all_to_all(expert_rows, group, 0, 0, tiled=True)
        slots = jnp.arange(EXPERTS * CAP, dtype=jnp.int32)
        combine = jnp.sum(
            jnp.where(
                position.reshape(tokens, TOP)[:, :, None] == slots[None, None, :],
                route_gates[0][:, :, None],
                0.0,
            ),
            axis=1,
        )
        expert_mix = jnp.dot(
            combine,
            returned.reshape(EXPERTS * CAP, D).astype(jnp.float32),
            precision=lax.Precision.HIGHEST,
        )
        return (mixed_wide + expert_mix).astype(jnp.bfloat16)[None]

    return shards


def solution(mesh):
    seq = ("seq_hi", "seq_lo")
    placed = (
        P("ep", seq, None),
        P("ep", seq, None),
        P("ep", seq, None),
        P("ep", seq, None),
        P("ep", None, None, None),
        P(),
        P(),
        P("ep", seq, None),
        P("ep", seq, None),
        P("ep", seq, None),
        P("ep", seq, None),
        P("ep", None, seq),
    )
    n_seq, n_ep = mesh.shape["seq"], mesh.shape["ep"]
    n_lo = EXPERTS // n_ep
    names = list(mesh.axis_names)
    shape, split_names = [], []
    for name in names:
        shape += [n_seq // n_lo, n_lo] if name == "seq" else [mesh.shape[name]]
        split_names += list(seq) if name == "seq" else [name]
    split = Mesh(mesh.devices.reshape(shape), tuple(split_names))
    return jax.shard_map(
        make_shards(n_seq), mesh=split, in_specs=placed, out_specs=P("ep", seq, None),
        check_vma=False,
    )
```

```python
import jax
import jax.numpy as jnp
from jax import lax
from jax.sharding import Mesh, PartitionSpec as P

D = 2048
HEADS = 16
HEAD_DIM = 128
EXPERTS = 16
TOP = 6
CAP = 50


def carried_in(array, axis, count):
    total = array
    shift = 1
    while shift < count:
        moved = lax.ppermute(total, axis, [(i, i + shift) for i in range(count - shift)])
        total = total + moved
        shift *= 2
    return total - array


def route_slots(block_routes):
    chosen = (block_routes[:, None] == jnp.arange(EXPERTS, dtype=jnp.int32)[None, :]).astype(
        jnp.int32
    )
    counts = jnp.cumsum(chosen, axis=0) - 1
    return jnp.sum(chosen * counts, axis=1)


def silu_gate(gate_sum, up_sum):
    return gate_sum / (1.0 + jnp.exp(-gate_sum)) * up_sum


def make_shards(n_seq):
    seq = ("seq_hi", "seq_lo")
    group = ("ep", "seq_lo")

    def shards(
        queries,
        key_rows,
        value_rows,
        residual,
        state_start,
        head_gain,
        ffn_gain,
        routes,
        route_gates,
        gate_weight,
        up_weight,
        down_weight,
    ):
        def collect(weight):
            mine = lax.all_to_all(weight, "seq_lo", 0, 0, tiled=False)
            return lax.all_gather(mine, "seq_hi", axis=0, tiled=False)

        whole_gate = collect(gate_weight)
        whole_up = collect(up_weight)
        whole_down = collect(down_weight)
        whole_gate = whole_gate.reshape(-1, whole_gate.shape[-1])
        whole_up = whole_up.reshape(-1, whole_up.shape[-1])

        tokens = queries.shape[1]
        query_heads = queries[0].reshape(tokens, HEADS, HEAD_DIM)
        key_heads = key_rows[0].reshape(tokens, HEADS, HEAD_DIM)
        value_heads = value_rows[0].reshape(tokens, HEADS, HEAD_DIM)
        local_state = jnp.einsum(
            "thd,the->hde", key_heads, value_heads, preferred_element_type=jnp.float32
        )
        earlier = carried_in(local_state, seq, n_seq)
        state_before = state_start[0] + earlier
        causal = (
            jnp.arange(tokens, dtype=jnp.int32)[:, None]
            >= jnp.arange(tokens, dtype=jnp.int32)[None, :]
        )
        scores = jnp.einsum(
            "thd,shd->hts", query_heads, key_heads, preferred_element_type=jnp.float32
        )
        scores = jnp.where(causal[None], scores, 0.0).astype(jnp.bfloat16)
        in_block = jnp.einsum(
            "hts,she->the", scores, value_heads, preferred_element_type=jnp.float32
        )
        from_state = jnp.einsum(
            "thd,hde->the",
            query_heads.astype(jnp.float32),
            state_before,
            precision=lax.Precision.HIGHEST,
        )
        attended = from_state + in_block
        head_scale = lax.rsqrt(jnp.mean(attended * attended, axis=-1, keepdims=True) + 1e-05)
        head_normed = (attended * head_scale).reshape(tokens, D) * head_gain
        mixed_rows = (residual[0].astype(jnp.float32) + head_normed).astype(jnp.bfloat16)
        mixed_rows = lax.optimization_barrier(mixed_rows)
        mixed_wide = mixed_rows.astype(jnp.float32)
        row_scale = lax.rsqrt(jnp.mean(mixed_wide * mixed_wide, axis=-1, keepdims=True) + 1e-05)
        ffn_in = (mixed_wide * row_scale * ffn_gain).astype(jnp.bfloat16)
        flat_routes = routes[0].reshape(-1)
        slot_rank = route_slots(flat_routes)
        position = flat_routes * CAP + slot_rank
        slots = jnp.arange(EXPERTS * CAP, dtype=jnp.int32)
        routed = position.reshape(tokens, TOP)[:, :, None] == slots[None, None, :]
        chosen = jnp.any(routed, axis=1).astype(jnp.bfloat16)
        outgoing = jnp.einsum(
            "ts,td->sd", chosen, ffn_in, preferred_element_type=jnp.float32
        ).astype(jnp.bfloat16)
        outgoing = outgoing.reshape(EXPERTS, CAP, D)
        arrived = lax.all_to_all(outgoing, group, 0, 0, tiled=True)
        arrived = arrived.reshape(EXPERTS * CAP, D)
        gate_sum = jnp.dot(arrived, whole_gate, preferred_element_type=jnp.float32)
        up_sum = jnp.dot(arrived, whole_up, preferred_element_type=jnp.float32)
        hidden = silu_gate(gate_sum, up_sum).astype(jnp.bfloat16)
        expert_rows = jnp.einsum(
            "rh,abhd->rabd", hidden, whole_down, preferred_element_type=jnp.float32
        ).astype(jnp.bfloat16)
        expert_rows = expert_rows.reshape(EXPERTS, CAP, D)
        returned = lax.all_to_all(expert_rows, group, 0, 0, tiled=True)
        combine = jnp.sum(jnp.where(routed, route_gates[0][:, :, None], 0.0), axis=1)
        expert_mix = jnp.dot(
            combine,
            returned.reshape(EXPERTS * CAP, D).astype(jnp.float32),
            precision=lax.Precision.HIGHEST,
        )
        return (mixed_wide + expert_mix).astype(jnp.bfloat16)[None]

    return shards


def solution(mesh):
    seq = ("seq_hi", "seq_lo")
    placed = (
        P("ep", seq, None),
        P("ep", seq, None),
        P("ep", seq, None),
        P("ep", seq, None),
        P("ep", None, None, None),
        P(),
        P(),
        P("ep", seq, None),
        P("ep", seq, None),
        P("ep", seq, None),
        P("ep", seq, None),
        P("ep", None, seq),
    )
    n_seq, n_ep = mesh.shape["seq"], mesh.shape["ep"]
    n_lo = EXPERTS // n_ep
    names = list(mesh.axis_names)
    shape, split_names = [], []
    for name in names:
        shape += [n_seq // n_lo, n_lo] if name == "seq" else [mesh.shape[name]]
        split_names += list(seq) if name == "seq" else [name]
    split = Mesh(mesh.devices.reshape(shape), tuple(split_names))
    return jax.shard_map(
        make_shards(n_seq), mesh=split, in_specs=placed, out_specs=P("ep", seq, None),
        check_vma=False,
    )
```

```python
import jax
import jax.numpy as jnp
from jax import lax
from jax.sharding import Mesh, PartitionSpec as P

D = 2048
HEADS = 16
HEAD_DIM = 128
EXPERTS = 16
TOP = 6
CAP = 50


def carried_in(array, axis, count):
    total = array
    shift = 1
    while shift < count:
        moved = lax.ppermute(total, axis, [(i, i + shift) for i in range(count - shift)])
        total = total + moved
        shift *= 2
    return total - array


def route_slots(block_routes):
    chosen = (block_routes[:, None] == jnp.arange(EXPERTS, dtype=jnp.int32)[None, :]).astype(
        jnp.int32
    )
    counts = jnp.cumsum(chosen, axis=0) - 1
    return jnp.sum(chosen * counts, axis=1)


def silu_gate(gate_sum, up_sum):
    return gate_sum / (1.0 + jnp.exp(-gate_sum)) * up_sum


def make_shards(n_seq):
    seq = ("seq_hi", "seq_lo")
    group = ("ep", "seq_lo")

    def shards(
        queries,
        key_rows,
        value_rows,
        residual,
        state_start,
        head_gain,
        ffn_gain,
        routes,
        route_gates,
        gate_weight,
        up_weight,
        down_weight,
    ):
        def collect(weight):
            mine = lax.all_to_all(weight, "seq_lo", 0, 0, tiled=False)
            return lax.all_gather(mine, "seq_hi", axis=0, tiled=False)

        whole_gate = collect(gate_weight)
        whole_up = collect(up_weight)
        whole_down = collect(down_weight)
        whole_gate = whole_gate.reshape(-1, whole_gate.shape[-1])
        whole_up = whole_up.reshape(-1, whole_up.shape[-1])

        tokens = queries.shape[1]
        query_heads = queries[0].reshape(tokens, HEADS, HEAD_DIM)
        key_heads = key_rows[0].reshape(tokens, HEADS, HEAD_DIM)
        value_heads = value_rows[0].reshape(tokens, HEADS, HEAD_DIM)
        local_state = jnp.einsum(
            "thd,the->hde", key_heads, value_heads, preferred_element_type=jnp.float32
        )
        earlier = carried_in(local_state, seq, n_seq)
        state_before = state_start[0] + earlier
        causal = (
            jnp.arange(tokens, dtype=jnp.int32)[:, None]
            >= jnp.arange(tokens, dtype=jnp.int32)[None, :]
        )
        scores = jnp.einsum(
            "thd,shd->hts", query_heads, key_heads, preferred_element_type=jnp.float32
        )
        scores = jnp.where(causal[None], scores, 0.0).astype(jnp.bfloat16)
        in_block = jnp.einsum(
            "hts,she->the", scores, value_heads, preferred_element_type=jnp.float32
        )
        from_state = jnp.einsum(
            "thd,hde->the",
            query_heads.astype(jnp.float32),
            state_before,
            precision=lax.Precision.HIGHEST,
        )
        attended = from_state + in_block
        head_scale = lax.rsqrt(jnp.mean(attended * attended, axis=-1, keepdims=True) + 1e-05)
        head_normed = (attended * head_scale).reshape(tokens, D) * head_gain
        mixed_rows = (residual[0].astype(jnp.float32) + head_normed).astype(jnp.bfloat16)
        mixed_rows = lax.optimization_barrier(mixed_rows)
        mixed_wide = mixed_rows.astype(jnp.float32)
        row_scale = lax.rsqrt(jnp.mean(mixed_wide * mixed_wide, axis=-1, keepdims=True) + 1e-05)
        ffn_in = (mixed_wide * row_scale * ffn_gain).astype(jnp.bfloat16)
        flat_routes = routes[0].reshape(-1)
        slot_rank = route_slots(flat_routes)
        position = flat_routes * CAP + slot_rank
        slots = jnp.arange(EXPERTS * CAP, dtype=jnp.int32)
        routed = position.reshape(tokens, TOP)[:, :, None] == slots[None, None, :]
        chosen = jnp.any(routed, axis=1).astype(jnp.bfloat16)
        outgoing = jnp.einsum(
            "ts,td->sd", chosen, ffn_in, preferred_element_type=jnp.float32
        ).astype(jnp.bfloat16)
        outgoing = outgoing.reshape(EXPERTS, CAP, D)
        outgoing, whole_gate, whole_up, whole_down = lax.optimization_barrier(
            (outgoing, whole_gate, whole_up, whole_down)
        )
        arrived = lax.all_to_all(outgoing, group, 0, 0, tiled=True)
        arrived = arrived.reshape(EXPERTS * CAP, D)
        gate_sum = jnp.dot(arrived, whole_gate, preferred_element_type=jnp.float32)
        up_sum = jnp.dot(arrived, whole_up, preferred_element_type=jnp.float32)
        hidden = silu_gate(gate_sum, up_sum).astype(jnp.bfloat16)
        expert_rows = jnp.einsum(
            "rh,abhd->rabd", hidden, whole_down, preferred_element_type=jnp.float32
        ).astype(jnp.bfloat16)
        expert_rows = expert_rows.reshape(EXPERTS, CAP, D)
        returned = lax.all_to_all(expert_rows, group, 0, 0, tiled=True)
        combine = jnp.sum(jnp.where(routed, route_gates[0][:, :, None], 0.0), axis=1)
        expert_mix = jnp.dot(
            combine,
            returned.reshape(EXPERTS * CAP, D).astype(jnp.float32),
            precision=lax.Precision.HIGHEST,
        )
        return (mixed_wide + expert_mix).astype(jnp.bfloat16)[None]

    return shards


def solution(mesh):
    seq = ("seq_hi", "seq_lo")
    placed = (
        P("ep", seq, None),
        P("ep", seq, None),
        P("ep", seq, None),
        P("ep", seq, None),
        P("ep", None, None, None),
        P(),
        P(),
        P("ep", seq, None),
        P("ep", seq, None),
        P("ep", seq, None),
        P("ep", seq, None),
        P("ep", None, seq),
    )
    n_seq, n_ep = mesh.shape["seq"], mesh.shape["ep"]
    n_lo = EXPERTS // n_ep
    names = list(mesh.axis_names)
    shape, split_names = [], []
    for name in names:
        shape += [n_seq // n_lo, n_lo] if name == "seq" else [mesh.shape[name]]
        split_names += list(seq) if name == "seq" else [name]
    split = Mesh(mesh.devices.reshape(shape), tuple(split_names))
    return jax.shard_map(
        make_shards(n_seq), mesh=split, in_specs=placed, out_specs=P("ep", seq, None),
        check_vma=False,
    )
```

```python
import jax
import jax.numpy as jnp
from jax import lax
from jax.sharding import Mesh, PartitionSpec as P

D = 2048
HEADS = 16
HEAD_DIM = 128
EXPERTS = 16
TOP = 6
CAP = 50


def carried_in(array, axis, count):
    total = array
    shift = 1
    while shift < count:
        moved = lax.ppermute(total, axis, [(i, i + shift) for i in range(count - shift)])
        total = total + moved
        shift *= 2
    return total - array


def route_slots(block_routes):
    chosen = (block_routes[:, None] == jnp.arange(EXPERTS, dtype=jnp.int32)[None, :]).astype(
        jnp.int32
    )
    counts = jnp.cumsum(chosen, axis=0) - 1
    return jnp.sum(chosen * counts, axis=1)


def silu_gate(gate_sum, up_sum):
    return gate_sum / (1.0 + jnp.exp(-gate_sum)) * up_sum


def make_shards(n_seq):
    seq = ("seq_hi", "seq_lo")
    group = ("ep", "seq_lo")

    def shards(
        queries,
        key_rows,
        value_rows,
        residual,
        state_start,
        head_gain,
        ffn_gain,
        routes,
        route_gates,
        gate_weight,
        up_weight,
        down_weight,
    ):
        def collect(weight):
            mine = lax.all_to_all(weight, "seq_lo", 0, 0, tiled=False)
            return lax.all_gather(mine, "seq_hi", axis=0, tiled=False)

        whole_gate = collect(gate_weight)
        whole_up = collect(up_weight)
        whole_down = collect(down_weight)
        whole_gate = whole_gate.reshape(-1, whole_gate.shape[-1])
        whole_up = whole_up.reshape(-1, whole_up.shape[-1])

        tokens = queries.shape[1]
        query_heads = queries[0].reshape(tokens, HEADS, HEAD_DIM)
        key_heads = key_rows[0].reshape(tokens, HEADS, HEAD_DIM)
        value_heads = value_rows[0].reshape(tokens, HEADS, HEAD_DIM)
        local_state = jnp.einsum(
            "thd,the->hde", key_heads, value_heads, preferred_element_type=jnp.float32
        )
        earlier = carried_in(local_state, seq, n_seq)
        state_before = state_start[0] + earlier
        causal = (
            jnp.arange(tokens, dtype=jnp.int32)[:, None]
            >= jnp.arange(tokens, dtype=jnp.int32)[None, :]
        )
        scores = jnp.einsum(
            "thd,shd->hts", query_heads, key_heads, preferred_element_type=jnp.float32
        )
        scores = jnp.where(causal[None], scores, 0.0).astype(jnp.bfloat16)
        in_block = jnp.einsum(
            "hts,she->the", scores, value_heads, preferred_element_type=jnp.float32
        )
        from_state = jnp.einsum(
            "thd,hde->the",
            query_heads.astype(jnp.float32),
            state_before,
            precision=lax.Precision.HIGHEST,
        )
        attended = from_state + in_block
        head_scale = lax.rsqrt(jnp.mean(attended * attended, axis=-1, keepdims=True) + 1e-05)
        head_normed = (attended * head_scale).reshape(tokens, D) * head_gain
        mixed_rows = (residual[0].astype(jnp.float32) + head_normed).astype(jnp.bfloat16)
        mixed_rows = lax.optimization_barrier(mixed_rows)
        mixed_wide = mixed_rows.astype(jnp.float32)
        row_scale = lax.rsqrt(jnp.mean(mixed_wide * mixed_wide, axis=-1, keepdims=True) + 1e-05)
        ffn_in = (mixed_wide * row_scale * ffn_gain).astype(jnp.bfloat16)
        flat_routes = routes[0].reshape(-1)
        slot_rank = route_slots(flat_routes)
        position = flat_routes * CAP + slot_rank
        slots = jnp.arange(EXPERTS * CAP, dtype=jnp.int32)
        routed = position.reshape(tokens, TOP)[:, :, None] == slots[None, None, :]
        chosen = jnp.any(routed, axis=1).astype(jnp.bfloat16)
        outgoing = jnp.einsum(
            "ts,td->sd", chosen, ffn_in, preferred_element_type=jnp.float32
        ).astype(jnp.bfloat16)
        outgoing = outgoing.reshape(EXPERTS, CAP, D)
        arrived = lax.all_to_all(outgoing, group, 0, 0, tiled=True)
        arrived = arrived.reshape(EXPERTS * CAP, D)
        gate_sum = jnp.dot(arrived, whole_gate, preferred_element_type=jnp.float32)
        up_sum = jnp.dot(arrived, whole_up, preferred_element_type=jnp.float32)
        hidden = silu_gate(gate_sum, up_sum).astype(jnp.bfloat16)
        down_rows = jnp.transpose(whole_down, (2, 0, 1, 3)).reshape(whole_down.shape[2], D)
        expert_rows = jnp.dot(
            hidden, down_rows, preferred_element_type=jnp.float32
        ).astype(jnp.bfloat16)
        expert_rows = expert_rows.reshape(EXPERTS, CAP, D)
        returned = lax.all_to_all(expert_rows, group, 0, 0, tiled=True)
        combine = jnp.sum(jnp.where(routed, route_gates[0][:, :, None], 0.0), axis=1)
        expert_mix = jnp.dot(
            combine,
            returned.reshape(EXPERTS * CAP, D).astype(jnp.float32),
            precision=lax.Precision.HIGHEST,
        )
        return (mixed_wide + expert_mix).astype(jnp.bfloat16)[None]

    return shards


def solution(mesh):
    seq = ("seq_hi", "seq_lo")
    placed = (
        P("ep", seq, None),
        P("ep", seq, None),
        P("ep", seq, None),
        P("ep", seq, None),
        P("ep", None, None, None),
        P(),
        P(),
        P("ep", seq, None),
        P("ep", seq, None),
        P("ep", seq, None),
        P("ep", seq, None),
        P("ep", None, seq),
    )
    n_seq, n_ep = mesh.shape["seq"], mesh.shape["ep"]
    n_lo = EXPERTS // n_ep
    names = list(mesh.axis_names)
    shape, split_names = [], []
    for name in names:
        shape += [n_seq // n_lo, n_lo] if name == "seq" else [mesh.shape[name]]
        split_names += list(seq) if name == "seq" else [name]
    split = Mesh(mesh.devices.reshape(shape), tuple(split_names))
    return jax.shard_map(
        make_shards(n_seq), mesh=split, in_specs=placed, out_specs=P("ep", seq, None),
        check_vma=False,
    )
```

```python
import jax
import jax.numpy as jnp
from jax import lax
from jax.sharding import Mesh, PartitionSpec as P

D = 2048
HEADS = 16
HEAD_DIM = 128
EXPERTS = 16
TOP = 6
CAP = 50


def carried_in(array, axis, count):
    total = array
    shift = 1
    while shift < count:
        moved = lax.ppermute(
            total.astype(jnp.bfloat16), axis, [(i, i + shift) for i in range(count - shift)]
        )
        total = total + moved.astype(jnp.float32)
        shift *= 2
    return total - array


def route_slots(block_routes):
    chosen = (block_routes[:, None] == jnp.arange(EXPERTS, dtype=jnp.int32)[None, :]).astype(
        jnp.int32
    )
    counts = jnp.cumsum(chosen, axis=0) - 1
    return jnp.sum(chosen * counts, axis=1)


def silu_gate(gate_sum, up_sum):
    return gate_sum / (1.0 + jnp.exp(-gate_sum)) * up_sum


def make_shards(n_seq):
    seq = ("seq_hi", "seq_lo")
    group = ("ep", "seq_lo")

    def shards(
        queries,
        key_rows,
        value_rows,
        residual,
        state_start,
        head_gain,
        ffn_gain,
        routes,
        route_gates,
        gate_weight,
        up_weight,
        down_weight,
    ):
        def collect(weight):
            mine = lax.all_to_all(weight, "seq_lo", 0, 0, tiled=False)
            return lax.all_gather(mine, "seq_hi", axis=0, tiled=False)

        whole_gate = collect(gate_weight)
        whole_up = collect(up_weight)
        whole_down = collect(down_weight)
        whole_gate = whole_gate.reshape(-1, whole_gate.shape[-1])
        whole_up = whole_up.reshape(-1, whole_up.shape[-1])

        tokens = queries.shape[1]
        query_heads = queries[0].reshape(tokens, HEADS, HEAD_DIM)
        key_heads = key_rows[0].reshape(tokens, HEADS, HEAD_DIM)
        value_heads = value_rows[0].reshape(tokens, HEADS, HEAD_DIM)
        local_state = jnp.einsum(
            "thd,the->hde", key_heads, value_heads, preferred_element_type=jnp.float32
        )
        earlier = carried_in(local_state, seq, n_seq)
        state_before = state_start[0] + earlier
        causal = (
            jnp.arange(tokens, dtype=jnp.int32)[:, None]
            >= jnp.arange(tokens, dtype=jnp.int32)[None, :]
        )
        scores = jnp.einsum(
            "thd,shd->hts", query_heads, key_heads, preferred_element_type=jnp.float32
        )
        scores = jnp.where(causal[None], scores, 0.0).astype(jnp.bfloat16)
        in_block = jnp.einsum(
            "hts,she->the", scores, value_heads, preferred_element_type=jnp.float32
        )
        from_state = jnp.einsum(
            "thd,hde->the",
            query_heads.astype(jnp.float32),
            state_before,
            precision=lax.Precision.HIGHEST,
        )
        attended = from_state + in_block
        head_scale = lax.rsqrt(jnp.mean(attended * attended, axis=-1, keepdims=True) + 1e-05)
        head_normed = (attended * head_scale).reshape(tokens, D) * head_gain
        mixed_rows = (residual[0].astype(jnp.float32) + head_normed).astype(jnp.bfloat16)
        mixed_rows = lax.optimization_barrier(mixed_rows)
        mixed_wide = mixed_rows.astype(jnp.float32)
        row_scale = lax.rsqrt(jnp.mean(mixed_wide * mixed_wide, axis=-1, keepdims=True) + 1e-05)
        ffn_in = (mixed_wide * row_scale * ffn_gain).astype(jnp.bfloat16)
        flat_routes = routes[0].reshape(-1)
        slot_rank = route_slots(flat_routes)
        position = flat_routes * CAP + slot_rank
        slots = jnp.arange(EXPERTS * CAP, dtype=jnp.int32)
        routed = position.reshape(tokens, TOP)[:, :, None] == slots[None, None, :]
        chosen = jnp.any(routed, axis=1).astype(jnp.bfloat16)
        outgoing = jnp.einsum(
            "ts,td->sd", chosen, ffn_in, preferred_element_type=jnp.float32
        ).astype(jnp.bfloat16)
        outgoing = outgoing.reshape(EXPERTS, CAP, D)
        arrived = lax.all_to_all(outgoing, group, 0, 0, tiled=True)
        arrived = arrived.reshape(EXPERTS * CAP, D)
        gate_sum = jnp.dot(arrived, whole_gate, preferred_element_type=jnp.float32)
        up_sum = jnp.dot(arrived, whole_up, preferred_element_type=jnp.float32)
        hidden = silu_gate(gate_sum, up_sum).astype(jnp.bfloat16)
        expert_rows = jnp.einsum(
            "rh,abhd->rabd", hidden, whole_down, preferred_element_type=jnp.float32
        ).astype(jnp.bfloat16)
        expert_rows = expert_rows.reshape(EXPERTS, CAP, D)
        returned = lax.all_to_all(expert_rows, group, 0, 0, tiled=True)
        combine = jnp.sum(jnp.where(routed, route_gates[0][:, :, None], 0.0), axis=1)
        expert_mix = jnp.dot(
            combine,
            returned.reshape(EXPERTS * CAP, D).astype(jnp.float32),
            precision=lax.Precision.HIGHEST,
        )
        return (mixed_wide + expert_mix).astype(jnp.bfloat16)[None]

    return shards


def solution(mesh):
    seq = ("seq_hi", "seq_lo")
    placed = (
        P("ep", seq, None),
        P("ep", seq, None),
        P("ep", seq, None),
        P("ep", seq, None),
        P("ep", None, None, None),
        P(),
        P(),
        P("ep", seq, None),
        P("ep", seq, None),
        P("ep", seq, None),
        P("ep", seq, None),
        P("ep", None, seq),
    )
    n_seq, n_ep = mesh.shape["seq"], mesh.shape["ep"]
    n_lo = EXPERTS // n_ep
    names = list(mesh.axis_names)
    shape, split_names = [], []
    for name in names:
        shape += [n_seq // n_lo, n_lo] if name == "seq" else [mesh.shape[name]]
        split_names += list(seq) if name == "seq" else [name]
    split = Mesh(mesh.devices.reshape(shape), tuple(split_names))
    return jax.shard_map(
        make_shards(n_seq), mesh=split, in_specs=placed, out_specs=P("ep", seq, None),
        check_vma=False,
    )
```

```python
import jax
import jax.numpy as jnp
from jax import lax
from jax.sharding import Mesh, PartitionSpec as P

D = 2048
HEADS = 16
HEAD_DIM = 128
EXPERTS = 16
TOP = 6
CAP = 50


def scanned(array, axis, count):
    total = array
    shift = 1
    while shift < count:
        moved = lax.ppermute(
            total.astype(jnp.bfloat16), axis, [(i, i + shift) for i in range(count - shift)]
        )
        total = total + moved.astype(jnp.float32)
        shift *= 2
    return total


def summed(array, axis, count):
    total = array
    shift = 1
    while shift < count:
        moved = lax.ppermute(
            total.astype(jnp.bfloat16), axis, [(i, i ^ shift) for i in range(count)]
        )
        total = total + moved.astype(jnp.float32)
        shift *= 2
    return total


def carried_in(array, n_hi, n_lo):
    within = scanned(array, "seq_lo", n_lo) - array
    group_total = summed(array, "seq_lo", n_lo)
    before = scanned(group_total, "seq_hi", n_hi) - group_total
    return within + before


def route_slots(block_routes):
    chosen = (block_routes[:, None] == jnp.arange(EXPERTS, dtype=jnp.int32)[None, :]).astype(
        jnp.int32
    )
    counts = jnp.cumsum(chosen, axis=0) - 1
    return jnp.sum(chosen * counts, axis=1)


def silu_gate(gate_sum, up_sum):
    return gate_sum / (1.0 + jnp.exp(-gate_sum)) * up_sum


def make_shards(n_seq, n_lo):
    seq = ("seq_hi", "seq_lo")
    group = ("ep", "seq_lo")

    def shards(
        queries,
        key_rows,
        value_rows,
        residual,
        state_start,
        head_gain,
        ffn_gain,
        routes,
        route_gates,
        gate_weight,
        up_weight,
        down_weight,
    ):
        def collect(weight):
            mine = lax.all_to_all(weight, "seq_lo", 0, 0, tiled=False)
            return lax.all_gather(mine, "seq_hi", axis=0, tiled=False)

        whole_gate = collect(gate_weight)
        whole_up = collect(up_weight)
        whole_down = collect(down_weight)
        whole_gate = whole_gate.reshape(-1, whole_gate.shape[-1])
        whole_up = whole_up.reshape(-1, whole_up.shape[-1])

        tokens = queries.shape[1]
        query_heads = queries[0].reshape(tokens, HEADS, HEAD_DIM)
        key_heads = key_rows[0].reshape(tokens, HEADS, HEAD_DIM)
        value_heads = value_rows[0].reshape(tokens, HEADS, HEAD_DIM)
        local_state = jnp.einsum(
            "thd,the->hde", key_heads, value_heads, preferred_element_type=jnp.float32
        )
        earlier = carried_in(local_state, n_seq // n_lo, n_lo)
        state_before = state_start[0] + earlier
        causal = (
            jnp.arange(tokens, dtype=jnp.int32)[:, None]
            >= jnp.arange(tokens, dtype=jnp.int32)[None, :]
        )
        scores = jnp.einsum(
            "thd,shd->hts", query_heads, key_heads, preferred_element_type=jnp.float32
        )
        scores = jnp.where(causal[None], scores, 0.0).astype(jnp.bfloat16)
        in_block = jnp.einsum(
            "hts,she->the", scores, value_heads, preferred_element_type=jnp.float32
        )
        from_state = jnp.einsum(
            "thd,hde->the",
            query_heads.astype(jnp.float32),
            state_before,
            precision=lax.Precision.HIGHEST,
        )
        attended = from_state + in_block
        head_scale = lax.rsqrt(jnp.mean(attended * attended, axis=-1, keepdims=True) + 1e-05)
        head_normed = (attended * head_scale).reshape(tokens, D) * head_gain
        mixed_rows = (residual[0].astype(jnp.float32) + head_normed).astype(jnp.bfloat16)
        mixed_rows = lax.optimization_barrier(mixed_rows)
        mixed_wide = mixed_rows.astype(jnp.float32)
        row_scale = lax.rsqrt(jnp.mean(mixed_wide * mixed_wide, axis=-1, keepdims=True) + 1e-05)
        ffn_in = (mixed_wide * row_scale * ffn_gain).astype(jnp.bfloat16)
        flat_routes = routes[0].reshape(-1)
        slot_rank = route_slots(flat_routes)
        position = flat_routes * CAP + slot_rank
        slots = jnp.arange(EXPERTS * CAP, dtype=jnp.int32)
        routed = position.reshape(tokens, TOP)[:, :, None] == slots[None, None, :]
        chosen = jnp.any(routed, axis=1).astype(jnp.bfloat16)
        outgoing = jnp.einsum(
            "ts,td->sd", chosen, ffn_in, preferred_element_type=jnp.float32
        ).astype(jnp.bfloat16)
        outgoing = outgoing.reshape(EXPERTS, CAP, D)
        arrived = lax.all_to_all(outgoing, group, 0, 0, tiled=True)
        arrived = arrived.reshape(EXPERTS * CAP, D)
        gate_sum = jnp.dot(arrived, whole_gate, preferred_element_type=jnp.float32)
        up_sum = jnp.dot(arrived, whole_up, preferred_element_type=jnp.float32)
        hidden = silu_gate(gate_sum, up_sum).astype(jnp.bfloat16)
        expert_rows = jnp.einsum(
            "rh,abhd->rabd", hidden, whole_down, preferred_element_type=jnp.float32
        ).astype(jnp.bfloat16)
        expert_rows = expert_rows.reshape(EXPERTS, CAP, D)
        returned = lax.all_to_all(expert_rows, group, 0, 0, tiled=True)
        combine = jnp.sum(jnp.where(routed, route_gates[0][:, :, None], 0.0), axis=1)
        expert_mix = jnp.dot(
            combine,
            returned.reshape(EXPERTS * CAP, D).astype(jnp.float32),
            precision=lax.Precision.HIGHEST,
        )
        return (mixed_wide + expert_mix).astype(jnp.bfloat16)[None]

    return shards


def solution(mesh):
    seq = ("seq_hi", "seq_lo")
    placed = (
        P("ep", seq, None),
        P("ep", seq, None),
        P("ep", seq, None),
        P("ep", seq, None),
        P("ep", None, None, None),
        P(),
        P(),
        P("ep", seq, None),
        P("ep", seq, None),
        P("ep", seq, None),
        P("ep", seq, None),
        P("ep", None, seq),
    )
    n_seq, n_ep = mesh.shape["seq"], mesh.shape["ep"]
    n_lo = EXPERTS // n_ep
    names = list(mesh.axis_names)
    shape, split_names = [], []
    for name in names:
        shape += [n_seq // n_lo, n_lo] if name == "seq" else [mesh.shape[name]]
        split_names += list(seq) if name == "seq" else [name]
    split = Mesh(mesh.devices.reshape(shape), tuple(split_names))
    return jax.shard_map(
        make_shards(n_seq, n_lo), mesh=split, in_specs=placed, out_specs=P("ep", seq, None),
        check_vma=False,
    )
```

```python
import jax
import jax.numpy as jnp
from jax import lax
from jax.sharding import Mesh, PartitionSpec as P

D = 2048
HEADS = 16
HEAD_DIM = 128
EXPERTS = 16
TOP = 6
CAP = 50


def carried_in(array, axis, count):
    total = array
    shift = 1
    while shift < count:
        moved = lax.ppermute(
            total.astype(jnp.bfloat16), axis, [(i, i + shift) for i in range(count - shift)]
        )
        total = total + moved.astype(jnp.float32)
        shift *= 2
    return total - array


def route_slots(block_routes):
    chosen = (block_routes[:, None] == jnp.arange(EXPERTS, dtype=jnp.int32)[None, :]).astype(
        jnp.int32
    )
    counts = jnp.cumsum(chosen, axis=0) - 1
    return jnp.sum(chosen * counts, axis=1)


def silu_gate(gate_sum, up_sum):
    return gate_sum / (1.0 + jnp.exp(-gate_sum)) * up_sum


def make_shards(n_seq):
    seq = ("seq_hi", "seq_lo")
    group = ("ep", "seq_lo")

    def shards(
        queries,
        key_rows,
        value_rows,
        residual,
        state_start,
        head_gain,
        ffn_gain,
        routes,
        route_gates,
        gate_weight,
        up_weight,
        down_weight,
    ):
        def collect(weight):
            mine = lax.all_to_all(weight, "seq_lo", 0, 0, tiled=False)
            return lax.all_gather(mine, "seq_hi", axis=0, tiled=False)

        whole_gate = collect(gate_weight)
        whole_up = collect(up_weight)
        down_mine = lax.all_to_all(down_weight, "seq_lo", 0, 0, tiled=False)
        whole_down = lax.all_gather(down_mine, "seq_hi", axis=0, tiled=False)
        whole_gate = whole_gate.reshape(-1, whole_gate.shape[-1])
        whole_up = whole_up.reshape(-1, whole_up.shape[-1])

        tokens = queries.shape[1]
        query_heads = queries[0].reshape(tokens, HEADS, HEAD_DIM)
        key_heads = key_rows[0].reshape(tokens, HEADS, HEAD_DIM)
        value_heads = value_rows[0].reshape(tokens, HEADS, HEAD_DIM)
        local_state = jnp.einsum(
            "thd,the->hde", key_heads, value_heads, preferred_element_type=jnp.float32
        )
        earlier = carried_in(local_state, seq, n_seq)
        state_before = state_start[0] + earlier
        causal = (
            jnp.arange(tokens, dtype=jnp.int32)[:, None]
            >= jnp.arange(tokens, dtype=jnp.int32)[None, :]
        )
        scores = jnp.einsum(
            "thd,shd->hts", query_heads, key_heads, preferred_element_type=jnp.float32
        )
        scores = jnp.where(causal[None], scores, 0.0).astype(jnp.bfloat16)
        in_block = jnp.einsum(
            "hts,she->the", scores, value_heads, preferred_element_type=jnp.float32
        )
        from_state = jnp.einsum(
            "thd,hde->the",
            query_heads.astype(jnp.float32),
            state_before,
            precision=lax.Precision.HIGHEST,
        )
        attended = from_state + in_block
        head_scale = lax.rsqrt(jnp.mean(attended * attended, axis=-1, keepdims=True) + 1e-05)
        head_normed = (attended * head_scale).reshape(tokens, D) * head_gain
        mixed_rows = (residual[0].astype(jnp.float32) + head_normed).astype(jnp.bfloat16)
        mixed_rows = lax.optimization_barrier(mixed_rows)
        mixed_wide = mixed_rows.astype(jnp.float32)
        row_scale = lax.rsqrt(jnp.mean(mixed_wide * mixed_wide, axis=-1, keepdims=True) + 1e-05)
        ffn_in = (mixed_wide * row_scale * ffn_gain).astype(jnp.bfloat16)
        flat_routes = routes[0].reshape(-1)
        slot_rank = route_slots(flat_routes)
        position = flat_routes * CAP + slot_rank
        slots = jnp.arange(EXPERTS * CAP, dtype=jnp.int32)
        routed = position.reshape(tokens, TOP)[:, :, None] == slots[None, None, :]
        chosen = jnp.any(routed, axis=1).astype(jnp.bfloat16)
        outgoing = jnp.einsum(
            "ts,td->sd", chosen, ffn_in, preferred_element_type=jnp.float32
        ).astype(jnp.bfloat16)
        outgoing = outgoing.reshape(EXPERTS, CAP, D)
        arrived = lax.all_to_all(outgoing, group, 0, 0, tiled=True)
        arrived = arrived.reshape(EXPERTS * CAP, D)
        gate_sum = jnp.dot(arrived, whole_gate, preferred_element_type=jnp.float32)
        up_sum = jnp.dot(arrived, whole_up, preferred_element_type=jnp.float32)
        hidden = silu_gate(gate_sum, up_sum).astype(jnp.bfloat16)
        if whole_down.shape[0] == 2:
            place = lax.axis_index("seq_hi")
            other = lax.dynamic_index_in_dim(whole_down, 1 - place, 0, False)
            own_rows = jnp.einsum(
                "rh,bhd->rbd", hidden, down_mine, preferred_element_type=jnp.float32
            )
            other_rows = jnp.einsum(
                "rh,bhd->rbd", hidden, other, preferred_element_type=jnp.float32
            )
            expert_rows = jnp.where(
                place == 0,
                jnp.stack([own_rows, other_rows], axis=1),
                jnp.stack([other_rows, own_rows], axis=1),
            ).astype(jnp.bfloat16)
        else:
            expert_rows = jnp.einsum(
                "rh,abhd->rabd", hidden, whole_down, preferred_element_type=jnp.float32
            ).astype(jnp.bfloat16)
        expert_rows = expert_rows.reshape(EXPERTS, CAP, D)
        returned = lax.all_to_all(expert_rows, group, 0, 0, tiled=True)
        combine = jnp.sum(jnp.where(routed, route_gates[0][:, :, None], 0.0), axis=1)
        expert_mix = jnp.dot(
            combine,
            returned.reshape(EXPERTS * CAP, D).astype(jnp.float32),
            precision=lax.Precision.HIGHEST,
        )
        return (mixed_wide + expert_mix).astype(jnp.bfloat16)[None]

    return shards


def solution(mesh):
    seq = ("seq_hi", "seq_lo")
    placed = (
        P("ep", seq, None),
        P("ep", seq, None),
        P("ep", seq, None),
        P("ep", seq, None),
        P("ep", None, None, None),
        P(),
        P(),
        P("ep", seq, None),
        P("ep", seq, None),
        P("ep", seq, None),
        P("ep", seq, None),
        P("ep", None, seq),
    )
    n_seq, n_ep = mesh.shape["seq"], mesh.shape["ep"]
    n_lo = EXPERTS // n_ep
    names = list(mesh.axis_names)
    shape, split_names = [], []
    for name in names:
        shape += [n_seq // n_lo, n_lo] if name == "seq" else [mesh.shape[name]]
        split_names += list(seq) if name == "seq" else [name]
    split = Mesh(mesh.devices.reshape(shape), tuple(split_names))
    return jax.shard_map(
        make_shards(n_seq), mesh=split, in_specs=placed, out_specs=P("ep", seq, None),
        check_vma=False,
    )
```

```python
import jax
import jax.numpy as jnp
from jax import lax
from jax.sharding import Mesh, PartitionSpec as P

D = 2048
HEADS = 16
HEAD_DIM = 128
EXPERTS = 16
TOP = 6
CAP = 50


def carried_in(array, axis, count):
    total = array
    shift = 1
    while shift < count:
        moved = lax.ppermute(
            total.astype(jnp.bfloat16), axis, [(i, i + shift) for i in range(count - shift)]
        )
        total = total + moved.astype(jnp.float32)
        shift *= 2
    return total - array


def route_slots(block_routes):
    chosen = (block_routes[:, None] == jnp.arange(EXPERTS, dtype=jnp.int32)[None, :]).astype(
        jnp.int32
    )
    counts = jnp.cumsum(chosen, axis=0) - 1
    return jnp.sum(chosen * counts, axis=1)


def silu_gate(gate_sum, up_sum):
    return gate_sum / (1.0 + jnp.exp(-gate_sum)) * up_sum


def make_shards(n_seq):
    seq = ("seq_hi", "seq_lo")
    group = ("ep", "seq_lo")

    def shards(
        queries,
        key_rows,
        value_rows,
        residual,
        state_start,
        head_gain,
        ffn_gain,
        routes,
        route_gates,
        gate_weight,
        up_weight,
        down_weight,
    ):
        def collect(weight):
            mine = lax.all_to_all(weight, "seq_lo", 0, 0, tiled=False)
            return lax.all_gather(mine, "seq_hi", axis=0, tiled=False)

        whole_gate = collect(gate_weight)
        whole_up = collect(up_weight)
        down_mine = lax.all_to_all(down_weight, "seq_lo", 0, 0, tiled=False)
        whole_down = lax.all_gather(down_mine, "seq_hi", axis=0, tiled=False)
        whole_gate = whole_gate.reshape(-1, whole_gate.shape[-1])
        whole_up = whole_up.reshape(-1, whole_up.shape[-1])

        tokens = queries.shape[1]
        query_heads = queries[0].reshape(tokens, HEADS, HEAD_DIM)
        key_heads = key_rows[0].reshape(tokens, HEADS, HEAD_DIM)
        value_heads = value_rows[0].reshape(tokens, HEADS, HEAD_DIM)
        local_state = jnp.einsum(
            "thd,the->hde", key_heads, value_heads, preferred_element_type=jnp.float32
        )
        earlier = carried_in(local_state, seq, n_seq)
        state_before = state_start[0] + earlier
        causal = (
            jnp.arange(tokens, dtype=jnp.int32)[:, None]
            >= jnp.arange(tokens, dtype=jnp.int32)[None, :]
        )
        scores = jnp.einsum(
            "thd,shd->hts", query_heads, key_heads, preferred_element_type=jnp.float32
        )
        scores = jnp.where(causal[None], scores, 0.0).astype(jnp.bfloat16)
        in_block = jnp.einsum(
            "hts,she->the", scores, value_heads, preferred_element_type=jnp.float32
        )
        from_state = jnp.einsum(
            "thd,hde->the",
            query_heads.astype(jnp.float32),
            state_before,
            precision=lax.Precision.HIGHEST,
        )
        attended = from_state + in_block
        head_scale = lax.rsqrt(jnp.mean(attended * attended, axis=-1, keepdims=True) + 1e-05)
        head_normed = (attended * head_scale).reshape(tokens, D) * head_gain
        mixed_rows = (residual[0].astype(jnp.float32) + head_normed).astype(jnp.bfloat16)
        mixed_rows = lax.optimization_barrier(mixed_rows)
        mixed_wide = mixed_rows.astype(jnp.float32)
        row_scale = lax.rsqrt(jnp.mean(mixed_wide * mixed_wide, axis=-1, keepdims=True) + 1e-05)
        ffn_in = (mixed_wide * row_scale * ffn_gain).astype(jnp.bfloat16)
        flat_routes = routes[0].reshape(-1)
        slot_rank = route_slots(flat_routes)
        position = flat_routes * CAP + slot_rank
        slots = jnp.arange(EXPERTS * CAP, dtype=jnp.int32)
        routed = position.reshape(tokens, TOP)[:, :, None] == slots[None, None, :]
        chosen = jnp.any(routed, axis=1).astype(jnp.bfloat16)
        outgoing = jnp.einsum(
            "ts,td->sd", chosen, ffn_in, preferred_element_type=jnp.float32
        ).astype(jnp.bfloat16)
        outgoing = outgoing.reshape(EXPERTS, CAP, D)
        arrived = lax.all_to_all(outgoing, group, 0, 0, tiled=True)
        arrived = arrived.reshape(EXPERTS * CAP, D)
        gate_sum = jnp.dot(arrived, whole_gate, preferred_element_type=jnp.float32)
        up_sum = jnp.dot(arrived, whole_up, preferred_element_type=jnp.float32)
        hidden = silu_gate(gate_sum, up_sum).astype(jnp.bfloat16)
        if whole_down.shape[0] == 2:
            place = lax.axis_index("seq_hi")
            other = lax.dynamic_index_in_dim(whole_down, 1 - place, 0, False)
            own_rows = jnp.einsum(
                "rh,bhd->rbd", hidden, down_mine, preferred_element_type=jnp.float32
            ).astype(jnp.bfloat16)
            other_rows = jnp.einsum(
                "rh,bhd->rbd", hidden, other, preferred_element_type=jnp.float32
            ).astype(jnp.bfloat16)
            own_back = lax.all_to_all(
                own_rows.reshape(EXPERTS, CAP, -1), group, 0, 0, tiled=True
            )
            other_back = lax.all_to_all(
                other_rows.reshape(EXPERTS, CAP, -1), group, 0, 0, tiled=True
            )
            returned = jnp.where(
                place == 0,
                jnp.concatenate([own_back, other_back], axis=2),
                jnp.concatenate([other_back, own_back], axis=2),
            )
        else:
            expert_rows = jnp.einsum(
                "rh,abhd->rabd", hidden, whole_down, preferred_element_type=jnp.float32
            ).astype(jnp.bfloat16)
            expert_rows = expert_rows.reshape(EXPERTS, CAP, D)
            returned = lax.all_to_all(expert_rows, group, 0, 0, tiled=True)
        combine = jnp.sum(jnp.where(routed, route_gates[0][:, :, None], 0.0), axis=1)
        expert_mix = jnp.dot(
            combine,
            returned.reshape(EXPERTS * CAP, D).astype(jnp.float32),
            precision=lax.Precision.HIGHEST,
        )
        return (mixed_wide + expert_mix).astype(jnp.bfloat16)[None]

    return shards


def solution(mesh):
    seq = ("seq_hi", "seq_lo")
    placed = (
        P("ep", seq, None),
        P("ep", seq, None),
        P("ep", seq, None),
        P("ep", seq, None),
        P("ep", None, None, None),
        P(),
        P(),
        P("ep", seq, None),
        P("ep", seq, None),
        P("ep", seq, None),
        P("ep", seq, None),
        P("ep", None, seq),
    )
    n_seq, n_ep = mesh.shape["seq"], mesh.shape["ep"]
    n_lo = EXPERTS // n_ep
    names = list(mesh.axis_names)
    shape, split_names = [], []
    for name in names:
        shape += [n_seq // n_lo, n_lo] if name == "seq" else [mesh.shape[name]]
        split_names += list(seq) if name == "seq" else [name]
    split = Mesh(mesh.devices.reshape(shape), tuple(split_names))
    return jax.shard_map(
        make_shards(n_seq), mesh=split, in_specs=placed, out_specs=P("ep", seq, None),
        check_vma=False,
    )
```
